32 devices in a mesh: space: 4 (over z), dp: 8 (over y, x, core).
Axes of the slice: x: 2, y: 2, z: 4, core: 2. Of those that a mesh axis runs over, the one named last changes fastest.
Arguments:
- features: bfloat16 [8, 12, 128, 320], P('dp', 'space'), may hold values from -6 to 6
- cotangent: bfloat16 [8, 12, 128, 320], P('dp', 'space'), may hold values from -6 to 6
- norm_gain: float32 [320], replicated, may hold values from 0.1 to 1.9
- norm_bias: float32 [320], replicated, may hold values from -0.5 to 0.5
- weight: bfloat16 [2880, 320], P('dp'), may hold values from -0.109375 to 0.109375
- moment_one: float32 [2880, 320], P('dp'), may hold values from -332.55374 to 332.55374
- moment_two: float32 [2880, 320], P('dp'), may hold values from 768 to 6144
- heights: int32 [8], P('dp'), may hold values from 6 to 12, as said below
- widths: int32 [8], P('dp'), may hold values from 64 to 128, as said below
Outputs:
- block_out: bfloat16 [8, 12, 128, 320], P('dp', 'space')
- input_grad: bfloat16 [8, 12, 128, 320], P('dp', 'space')
- weight_grad: float32 [2880, 320], P('dp')
- adam_update: float32 [2880, 320], P('dp')
The draws below stay inside these ranges and needn't reach their ends.
Inputs may be any that keep to these rules, and one draw needn't show every extreme that they name: Image i occupies canvas rows 0 to heights[i] - 1; some image has all 12 rows. Image i occupies canvas columns 0 to widths[i] - 1; some image has all 128 columns.
All inputs are finite; a program needn't handle non-finite values.
Results may differ from the reference program's by a relative error of at most 0.017.
Values may be sent and summed in bfloat16 or wider, within the bound.
No kernel may reach another device: no remote copies, remote signals or barrier semaphores. Data moves between devices by JAX's collectives and lax.ppermute only.
A program may use at most 64 MiB of HBM per device.

```python
import math
import jax
import jax.numpy as jnp
from jax import lax

C = 320
GROUPS = 32
WIDTH = 128
HEIGHT = 12
IMAGES = 8
KIN = 2880


def draw_heights(key, part):
    drawn = jax.random.randint(jax.random.fold_in(key, 11), (IMAGES,), HEIGHT // 2, HEIGHT + 1)
    return drawn.at[0].set(HEIGHT).astype(jnp.int32)


def draw_widths(key, part):
    drawn = jax.random.randint(jax.random.fold_in(key, 23), (IMAGES,), WIDTH // 2, WIDTH + 1)
    return drawn.at[IMAGES - 1].set(WIDTH).astype(jnp.int32)


def block_levels(own_key, shape, cuts, smallest, high):
    factor_of, own = 1.0, jax.random.fold_in(own_key, 6)
    for position, blocks in cuts:
        steps = jnp.exp(jax.random.uniform(jax.random.fold_in(own, position), (blocks,), jnp.float32, smallest / len(cuts), high / len(cuts)))
        factor_of = factor_of * jnp.repeat(steps, shape[position] // blocks).reshape([-1 if axis == position else 1 for axis in range(len(shape))])
    return factor_of


def scatter_about(rng, dims, deviation, reach, pieces=(), dtype=jnp.bfloat16):
    result = deviation * jax.random.normal(rng, dims, jnp.float32)
    if pieces:
        result = result * block_levels(rng, dims, pieces, -0.22, 0.18)
    return jnp.clip(result, -reach, reach).astype(dtype)


def setup_inputs(seed: int = 0) -> dict:
    seeds = jax.random.split(jax.random.key(seed), 10)
    return {
        "features": scatter_about(seeds[0], (IMAGES, HEIGHT, WIDTH, C), 1.0, 6.0, ((0, 8), (1, 4))),
        "cotangent": scatter_about(seeds[1], (IMAGES, HEIGHT, WIDTH, C), 1.0, 6.0, ((0, 8), (1, 4))),
        "norm_gain": jnp.clip(1.0 + 0.18 * jax.random.normal(seeds[2], (C,), jnp.float32), 0.1, 1.9),
        "norm_bias": jnp.clip(jax.random.uniform(seeds[3], (C,), jnp.float32, -0.5, 0.5), -0.5, 0.5),
        "weight": scatter_about(seeds[4], (KIN, C), KIN ** -0.5, 0.109375, ((0, 8),)),
        "moment_one": scatter_about(seeds[5], (KIN, C), (0.5 * (IMAGES * HEIGHT * WIDTH) ** 0.5), 332.55374, ((0, 8),), jnp.float32),
        "moment_two": jnp.clip(jnp.exp(math.log(6144.0) - 2.0794415 * jax.random.uniform(seeds[6], (KIN, C), jnp.float32) ** block_levels(seeds[6], (KIN, C), ((0, 8),), -0.2, 0.2)), 768.0, 6144.0),
        "heights": draw_heights(jax.random.fold_in(seeds[9], 71), 0),
        "widths": draw_widths(jax.random.fold_in(seeds[9], 71), 0),
    }


def group_sum(values, groups):
    height_dev, width_dev, channels = values.shape
    return values.reshape(height_dev, width_dev, groups, channels // groups).sum(axis=(0, 1, 3))

def spread_groups(statistic, channels):
    return jnp.repeat(statistic, channels // statistic.shape[0])

def reference(features, cotangent, norm_gain, norm_bias, weight, moment_one, moment_two, heights, widths):
    tap_weights = weight.reshape(9, C, C)

    def one_image(grad_total, item):
        latent, cot_image, height_img, width_img = item
        inside = ((jnp.arange(HEIGHT) < height_img)[:, None] & (jnp.arange(WIDTH) < width_img)[None, :]).astype(jnp.float32)[..., None]
        cell_count = (height_img * width_img * (C // GROUPS)).astype(jnp.float32)
        values = latent.astype(jnp.float32) * inside
        center = group_sum(values, GROUPS) / cell_count
        spread = group_sum(values * values, GROUPS) / cell_count - center * center
        inverse = lax.rsqrt(spread + 1e-05)
        normed = (values - spread_groups(center, C)) * spread_groups(inverse, C) * inside
        before = normed * norm_gain + norm_bias
        activated = (jax.nn.silu(before) * inside).astype(jnp.bfloat16)
        act_pad = jnp.pad(activated, ((1, 1), (1, 1), (0, 0)))
        masked = cot_image * inside.astype(jnp.bfloat16)
        cot_pad = jnp.pad(masked, ((1, 1), (1, 1), (0, 0)))
        flat_cot = masked.reshape(-1, C)
        output = jnp.zeros((HEIGHT * WIDTH, C), jnp.float32)
        upstream = jnp.zeros((HEIGHT * WIDTH, C), jnp.float32)
        tap_grads = []
        for row_off in range(3):
            for col_off in range(3):
                tap_index = row_off * 3 + col_off
                window = act_pad[row_off:row_off + HEIGHT, col_off:col_off + WIDTH].reshape(-1, C)
                output = output + jnp.dot(window, tap_weights[tap_index], preferred_element_type=jnp.float32)
                tap_grads.append(lax.dot_general(window, flat_cot, (((0,), (0,)), ((), ())), preferred_element_type=jnp.float32))
                cot_window = cot_pad[2 - row_off:2 - row_off + HEIGHT, 2 - col_off:2 - col_off + WIDTH].reshape(-1, C)
                upstream = upstream + lax.dot_general(cot_window, tap_weights[tap_index], (((1,), (1,)), ((), ())), preferred_element_type=jnp.float32)
        block_image = (output.reshape(HEIGHT, WIDTH, C) * inside).astype(jnp.bfloat16)
        gate_sig = jax.nn.sigmoid(before)
        silu_slope = gate_sig * (1.0 + before * (1.0 - gate_sig))
        scaled = upstream.reshape(HEIGHT, WIDTH, C) * silu_slope * inside * norm_gain
        first = group_sum(scaled, GROUPS) / cell_count
        second = group_sum(scaled * normed, GROUPS) / cell_count
        grad_image = (spread_groups(inverse, C) * (scaled - spread_groups(first, C) - normed * spread_groups(second, C)) * inside).astype(jnp.bfloat16)
        return (grad_total + jnp.stack(tap_grads), (block_image, grad_image))
    grad_total, (block_out, input_grad) = lax.scan(one_image, jnp.zeros((9, C, C), jnp.float32), (features, cotangent, heights, widths))
    weight_grad = grad_total.reshape(KIN, C)
    first_new = 0.9 * moment_one + 0.1 * weight_grad
    second_new = 0.999 * moment_two + 0.001 * weight_grad * weight_grad
    adam_update = first_new / (1.0 - 0.9 ** 10) / (jnp.sqrt(second_new / (1.0 - 0.999 ** 10)) + 1e-08)
    return (block_out, input_grad, weight_grad, adam_update)
```

```python
import jax
import jax.numpy as jnp
from jax import lax
from jax.sharding import PartitionSpec as P

GROUPS = 32


def with_halo(cells, sides, width):
    for axis, dim in sides:
        count = lax.axis_size(axis)
        ends = count - 1
        head = lax.slice_in_dim(cells, 0, width, axis=dim)
        tail = lax.slice_in_dim(cells, cells.shape[dim] - width, cells.shape[dim], axis=dim)
        cells = jnp.concatenate(
            [
                lax.ppermute(tail, axis, [(i, (i + 1) % count) for i in range(ends)]),
                cells,
                lax.ppermute(head, axis, [((i + 1) % count, i) for i in range(ends)]),
            ],
            axis=dim,
        )
    return cells


def space_sum(parts, axis):
    count = lax.axis_size(axis)
    if count & (count - 1):
        return lax.psum(parts, axis)
    step = 1
    while step < count:
        pairs = [(i, i ^ step) for i in range(count)]
        parts = tuple(p + q for p, q in zip(parts, lax.ppermute(parts, axis, pairs)))
        step *= 2
    return parts


def group_sum(values, groups):
    height_dev, width_dev, channels = values.shape
    return values.reshape(height_dev, width_dev, groups, channels // groups).sum(axis=(0, 1, 3))


def spread_groups(statistic, channels):
    return jnp.repeat(statistic, channels // statistic.shape[0])


def pad_columns(padded_rows):
    return jnp.pad(padded_rows, ((0, 0), (1, 1), (0, 0)))


def local(
    features, cotangent, norm_gain, norm_bias, weight, moment_one, moment_two, heights, widths
):
    latent = features[0]
    height_dev, width_dev, channels = latent.shape
    row_ids = lax.axis_index("space") * height_dev + jnp.arange(height_dev, dtype=jnp.int32)
    inside = (
        (row_ids < heights[0])[:, None]
        & (jnp.arange(width_dev, dtype=jnp.int32) < widths[0])[None, :]
    ).astype(jnp.float32)[..., None]
    cell_count = (heights[0] * widths[0] * (channels // GROUPS)).astype(jnp.float32)
    gathered = lax.all_gather(weight, "dp", axis=0, tiled=True)
    tap_weights = gathered.reshape(9, channels, channels)
    values = latent.astype(jnp.float32) * inside
    group_total, squares = space_sum(
        (group_sum(values, GROUPS), group_sum(values * values, GROUPS)), "space"
    )
    center = group_total / cell_count
    spread = squares / cell_count - center * center
    inverse = lax.rsqrt(spread + 1e-05)
    normed = (values - spread_groups(center, channels)) * spread_groups(inverse, channels) * inside
    before = normed * norm_gain + norm_bias
    activated = (jax.nn.silu(before) * inside).astype(jnp.bfloat16)
    act_pad = pad_columns(with_halo(activated, (("space", 0),), 1))
    output = jnp.zeros((height_dev * width_dev, channels), jnp.float32)
    for row_off in range(3):
        for col_off in range(3):
            window = act_pad[row_off : row_off + height_dev, col_off : col_off + width_dev].reshape(
                -1, channels
            )
            output = output + jnp.dot(
                window, tap_weights[row_off * 3 + col_off], preferred_element_type=jnp.float32
            )
    block_out = (output.reshape(height_dev, width_dev, channels) * inside).astype(jnp.bfloat16)
    masked = cotangent[0] * inside.astype(jnp.bfloat16)
    cot_pad = pad_columns(with_halo(masked, (("space", 0),), 1))
    flat_cot = masked.reshape(-1, channels)
    upstream = jnp.zeros((height_dev * width_dev, channels), jnp.float32)
    tap_grads = []
    for row_off in range(3):
        for col_off in range(3):
            tap_index = row_off * 3 + col_off
            window = act_pad[row_off : row_off + height_dev, col_off : col_off + width_dev].reshape(
                -1, channels
            )
            tap_grads.append(
                lax.dot_general(
                    window, flat_cot, (((0,), (0,)), ((), ())), preferred_element_type=jnp.float32
                )
            )
            cot_window = cot_pad[
                2 - row_off : 2 - row_off + height_dev, 2 - col_off : 2 - col_off + width_dev
            ].reshape(-1, channels)
            upstream = upstream + lax.dot_general(
                cot_window,
                tap_weights[tap_index],
                (((1,), (1,)), ((), ())),
                preferred_element_type=jnp.float32,
            )
    weight_terms = jnp.stack(tap_grads).reshape(9 * channels, channels)
    gate_sig = jax.nn.sigmoid(before)
    silu_slope = gate_sig * (1.0 + before * (1.0 - gate_sig))
    scaled = upstream.reshape(height_dev, width_dev, channels) * silu_slope * inside * norm_gain
    local_first = group_sum(scaled, GROUPS)
    local_second = group_sum(scaled * normed, GROUPS)
    dp_size = lax.axis_size("dp")
    grad_piece = lax.psum_scatter(
        weight_terms.astype(jnp.bfloat16).reshape(dp_size, -1, channels),
        "dp",
        scatter_dimension=0,
        tiled=False,
    )
    sum_first, sum_second = space_sum((local_first, local_second), "space")
    grad_piece = lax.psum(grad_piece, "space").astype(jnp.float32)
    first = sum_first / cell_count
    second = sum_second / cell_count
    input_grad = (
        spread_groups(inverse, channels)
        * (scaled - spread_groups(first, channels) - normed * spread_groups(second, channels))
        * inside
    ).astype(jnp.bfloat16)
    first_new = 0.9 * moment_one + 0.1 * grad_piece
    second_new = 0.999 * moment_two + 0.001 * grad_piece * grad_piece
    adam_update = first_new / (1.0 - 0.9**10) / (jnp.sqrt(second_new / (1.0 - 0.999**10)) + 1e-08)
    return (block_out[None], input_grad[None], grad_piece, adam_update)


def solution(mesh):
    placed = (
        P("dp", "space", None, None),
        P("dp", "space", None, None),
        P(),
        P(),
        P("dp", None),
        P("dp", None),
        P("dp", None),
        P("dp"),
        P("dp"),
    )
    return jax.shard_map(
        local,
        mesh=mesh,
        in_specs=placed,
        out_specs=(
            P("dp", "space", None, None),
            P("dp", "space", None, None),
            P("dp", None),
            P("dp", None),
        ),
        check_vma=False,
    )
```

```python
import jax
import jax.numpy as jnp
from jax import lax
from jax.sharding import PartitionSpec as P

GROUPS = 32


def with_halo(cells, sides, width):
    for axis, dim in sides:
        count = lax.axis_size(axis)
        ends = count - 1
        head = lax.slice_in_dim(cells, 0, width, axis=dim)
        tail = lax.slice_in_dim(cells, cells.shape[dim] - width, cells.shape[dim], axis=dim)
        cells = jnp.concatenate(
            [
                lax.ppermute(tail, axis, [(i, (i + 1) % count) for i in range(ends)]),
                cells,
                lax.ppermute(head, axis, [((i + 1) % count, i) for i in range(ends)]),
            ],
            axis=dim,
        )
    return cells


def space_sum(parts, axis):
    count = lax.axis_size(axis)
    if count & (count - 1):
        return lax.psum(parts, axis)
    step = 1
    while step < count:
        pairs = [(i, i ^ step) for i in range(count)]
        parts = tuple(p + q for p, q in zip(parts, lax.ppermute(parts, axis, pairs)))
        step *= 2
    return parts


def halving_scatter(partial, axis):
    count = lax.axis_size(axis)
    rows, channels = partial.shape[0] // count, partial.shape[1]
    if count & (count - 1):
        summed = lax.psum_scatter(
            partial.astype(jnp.bfloat16).reshape(count, rows, channels),
            axis,
            scatter_dimension=0,
            tiled=False,
        )
        return summed.astype(jnp.float32)
    index = lax.axis_index(axis)
    held = partial.reshape(count, rows, channels)
    step = 1
    while step < count:
        bit = (index // step) % 2
        paired = held.reshape(-1, 2, rows, channels)
        keep = lax.dynamic_index_in_dim(paired, bit, axis=1, keepdims=False)
        send = lax.dynamic_index_in_dim(paired, 1 - bit, axis=1, keepdims=False)
        pairs = [(i, i ^ step) for i in range(count)]
        got = lax.ppermute(send.astype(jnp.bfloat16), axis, pairs)
        held = keep + got.astype(jnp.float32)
        step *= 2
    return held[0]


def replicated_sum(value, axis):
    count = lax.axis_size(axis)
    if count & (count - 1):
        return lax.psum(value.astype(jnp.bfloat16), axis).astype(jnp.float32)
    step = 1
    while step < count:
        mine = value.astype(jnp.bfloat16)
        pairs = [(i, i ^ step) for i in range(count)]
        value = mine.astype(jnp.float32) + lax.ppermute(mine, axis, pairs).astype(jnp.float32)
        step *= 2
    return value


def group_sum(values, groups):
    height_dev, width_dev, channels = values.shape
    return values.reshape(height_dev, width_dev, groups, channels // groups).sum(axis=(0, 1, 3))


def spread_groups(statistic, channels):
    return jnp.repeat(statistic, channels // statistic.shape[0])


def pad_columns(padded_rows):
    return jnp.pad(padded_rows, ((0, 0), (1, 1), (0, 0)))


def local(
    features, cotangent, norm_gain, norm_bias, weight, moment_one, moment_two, heights, widths
):
    latent = features[0]
    height_dev, width_dev, channels = latent.shape
    row_ids = lax.axis_index("space") * height_dev + jnp.arange(height_dev, dtype=jnp.int32)
    inside = (
        (row_ids < heights[0])[:, None]
        & (jnp.arange(width_dev, dtype=jnp.int32) < widths[0])[None, :]
    ).astype(jnp.float32)[..., None]
    cell_count = (heights[0] * widths[0] * (channels // GROUPS)).astype(jnp.float32)
    gathered = lax.all_gather(weight, "dp", axis=0, tiled=True)
    tap_weights = gathered.reshape(9, channels, channels)
    values = latent.astype(jnp.float32) * inside
    group_total, squares = space_sum(
        (group_sum(values, GROUPS), group_sum(values * values, GROUPS)), "space"
    )
    center = group_total / cell_count
    spread = squares / cell_count - center * center
    inverse = lax.rsqrt(spread + 1e-05)
    normed = (values - spread_groups(center, channels)) * spread_groups(inverse, channels) * inside
    before = normed * norm_gain + norm_bias
    activated = (jax.nn.silu(before) * inside).astype(jnp.bfloat16)
    act_pad = pad_columns(with_halo(activated, (("space", 0),), 1))
    output = jnp.zeros((height_dev * width_dev, channels), jnp.float32)
    for row_off in range(3):
        for col_off in range(3):
            window = act_pad[row_off : row_off + height_dev, col_off : col_off + width_dev].reshape(
                -1, channels
            )
            output = output + jnp.dot(
                window, tap_weights[row_off * 3 + col_off], preferred_element_type=jnp.float32
            )
    block_out = (output.reshape(height_dev, width_dev, channels) * inside).astype(jnp.bfloat16)
    masked = cotangent[0] * inside.astype(jnp.bfloat16)
    cot_pad = pad_columns(with_halo(masked, (("space", 0),), 1))
    flat_cot = masked.reshape(-1, channels)
    upstream = jnp.zeros((height_dev * width_dev, channels), jnp.float32)
    tap_grads = []
    for row_off in range(3):
        for col_off in range(3):
            tap_index = row_off * 3 + col_off
            window = act_pad[row_off : row_off + height_dev, col_off : col_off + width_dev].reshape(
                -1, channels
            )
            tap_grads.append(
                lax.dot_general(
                    window, flat_cot, (((0,), (0,)), ((), ())), preferred_element_type=jnp.float32
                )
            )
            cot_window = cot_pad[
                2 - row_off : 2 - row_off + height_dev, 2 - col_off : 2 - col_off + width_dev
            ].reshape(-1, channels)
            upstream = upstream + lax.dot_general(
                cot_window,
                tap_weights[tap_index],
                (((1,), (1,)), ((), ())),
                preferred_element_type=jnp.float32,
            )
    weight_terms = jnp.stack(tap_grads).reshape(9 * channels, channels)
    gate_sig = jax.nn.sigmoid(before)
    silu_slope = gate_sig * (1.0 + before * (1.0 - gate_sig))
    scaled = upstream.reshape(height_dev, width_dev, channels) * silu_slope * inside * norm_gain
    local_first = group_sum(scaled, GROUPS)
    local_second = group_sum(scaled * normed, GROUPS)
    grad_piece = halving_scatter(weight_terms, "dp")
    sum_first, sum_second = space_sum((local_first, local_second), "space")
    grad_piece = replicated_sum(grad_piece, "space")
    first = sum_first / cell_count
    second = sum_second / cell_count
    input_grad = (
        spread_groups(inverse, channels)
        * (scaled - spread_groups(first, channels) - normed * spread_groups(second, channels))
        * inside
    ).astype(jnp.bfloat16)
    first_new = 0.9 * moment_one + 0.1 * grad_piece
    second_new = 0.999 * moment_two + 0.001 * grad_piece * grad_piece
    adam_update = first_new / (1.0 - 0.9**10) / (jnp.sqrt(second_new / (1.0 - 0.999**10)) + 1e-08)
    return (block_out[None], input_grad[None], grad_piece, adam_update)


def solution(mesh):
    placed = (
        P("dp", "space", None, None),
        P("dp", "space", None, None),
        P(),
        P(),
        P("dp", None),
        P("dp", None),
        P("dp", None),
        P("dp"),
        P("dp"),
    )
    return jax.shard_map(
        local,
        mesh=mesh,
        in_specs=placed,
        out_specs=(
            P("dp", "space", None, None),
            P("dp", "space", None, None),
            P("dp", None),
            P("dp", None),
        ),
        check_vma=False,
    )
```

```python
import jax
import jax.numpy as jnp
from jax import lax
from jax.sharding import PartitionSpec as P

GROUPS = 32


def with_halo(cells, sides, width):
    for axis, dim in sides:
        count = lax.axis_size(axis)
        ends = count - 1
        head = lax.slice_in_dim(cells, 0, width, axis=dim)
        tail = lax.slice_in_dim(cells, cells.shape[dim] - width, cells.shape[dim], axis=dim)
        cells = jnp.concatenate(
            [
                lax.ppermute(tail, axis, [(i, (i + 1) % count) for i in range(ends)]),
                cells,
                lax.ppermute(head, axis, [((i + 1) % count, i) for i in range(ends)]),
            ],
            axis=dim,
        )
    return cells


def space_sum(parts, axis):
    count = lax.axis_size(axis)
    if count > 4:
        return lax.psum(parts, axis)
    joined = jnp.stack(parts)
    shifted = [
        lax.ppermute(joined, axis, [(i, (i + shift) % count) for i in range(count)])
        for shift in range(1, count)
    ]
    for got in shifted:
        joined = joined + got
    return tuple(joined)


def halving_scatter(partial, axis):
    count = lax.axis_size(axis)
    rows, channels = partial.shape[0] // count, partial.shape[1]
    if count & (count - 1):
        summed = lax.psum_scatter(
            partial.astype(jnp.bfloat16).reshape(count, rows, channels),
            axis,
            scatter_dimension=0,
            tiled=False,
        )
        return summed.astype(jnp.float32)
    index = lax.axis_index(axis)
    held = partial.reshape(count, rows, channels)
    step = 1
    while step < count:
        bit = (index // step) % 2
        paired = held.reshape(-1, 2, rows, channels)
        keep = lax.dynamic_index_in_dim(paired, bit, axis=1, keepdims=False)
        send = lax.dynamic_index_in_dim(paired, 1 - bit, axis=1, keepdims=False)
        pairs = [(i, i ^ step) for i in range(count)]
        got = lax.ppermute(send.astype(jnp.bfloat16), axis, pairs)
        held = keep + got.astype(jnp.float32)
        step *= 2
    return held[0]


def replicated_sum(value, axis):
    count = lax.axis_size(axis)
    if count & (count - 1):
        return lax.psum(value.astype(jnp.bfloat16), axis).astype(jnp.float32)
    step = 1
    while step < count:
        mine = value.astype(jnp.bfloat16)
        pairs = [(i, i ^ step) for i in range(count)]
        value = mine.astype(jnp.float32) + lax.ppermute(mine, axis, pairs).astype(jnp.float32)
        step *= 2
    return value


def group_sum(values, groups):
    height_dev, width_dev, channels = values.shape
    return values.reshape(height_dev, width_dev, groups, channels // groups).sum(axis=(0, 1, 3))


def spread_groups(statistic, channels):
    return jnp.repeat(statistic, channels // statistic.shape[0])


def pad_columns(padded_rows):
    return jnp.pad(padded_rows, ((0, 0), (1, 1), (0, 0)))


def local(
    features, cotangent, norm_gain, norm_bias, weight, moment_one, moment_two, heights, widths
):
    latent = features[0]
    height_dev, width_dev, channels = latent.shape
    row_ids = lax.axis_index("space") * height_dev + jnp.arange(height_dev, dtype=jnp.int32)
    inside = (
        (row_ids < heights[0])[:, None]
        & (jnp.arange(width_dev, dtype=jnp.int32) < widths[0])[None, :]
    ).astype(jnp.float32)[..., None]
    cell_count = (heights[0] * widths[0] * (channels // GROUPS)).astype(jnp.float32)
    gathered = lax.all_gather(weight, "dp", axis=0, tiled=True)
    tap_weights = gathered.reshape(9, channels, channels)
    values = latent.astype(jnp.float32) * inside
    group_total, squares = space_sum(
        (group_sum(values, GROUPS), group_sum(values * values, GROUPS)), "space"
    )
    center = group_total / cell_count
    spread = squares / cell_count - center * center
    inverse = lax.rsqrt(spread + 1e-05)
    normed = (values - spread_groups(center, channels)) * spread_groups(inverse, channels) * inside
    before = normed * norm_gain + norm_bias
    activated = (jax.nn.silu(before) * inside).astype(jnp.bfloat16)
    act_pad = pad_columns(with_halo(activated, (("space", 0),), 1))
    act_cols = jnp.concatenate(
        [
            act_pad[row_off : row_off + height_dev, col_off : col_off + width_dev]
            for row_off in range(3)
            for col_off in range(3)
        ],
        axis=-1,
    ).reshape(height_dev * width_dev, 9 * channels)
    output = jnp.dot(act_cols, gathered, preferred_element_type=jnp.float32)
    block_out = (output.reshape(height_dev, width_dev, channels) * inside).astype(jnp.bfloat16)
    masked = cotangent[0] * inside.astype(jnp.bfloat16)
    cot_pad = pad_columns(with_halo(masked, (("space", 0),), 1))
    flat_cot = masked.reshape(-1, channels)
    weight_terms = lax.dot_general(
        act_cols, flat_cot, (((0,), (0,)), ((), ())), preferred_element_type=jnp.float32
    )
    cot_cols = jnp.concatenate(
        [
            cot_pad[2 - row_off : 2 - row_off + height_dev, 2 - col_off : 2 - col_off + width_dev]
            for row_off in range(3)
            for col_off in range(3)
        ],
        axis=-1,
    ).reshape(height_dev * width_dev, 9 * channels)
    flipped = tap_weights.transpose(0, 2, 1).reshape(9 * channels, channels)
    upstream = jnp.dot(cot_cols, flipped, preferred_element_type=jnp.float32)
    gate_sig = jax.nn.sigmoid(before)
    silu_slope = gate_sig * (1.0 + before * (1.0 - gate_sig))
    scaled = upstream.reshape(height_dev, width_dev, channels) * silu_slope * inside * norm_gain
    local_first = group_sum(scaled, GROUPS)
    local_second = group_sum(scaled * normed, GROUPS)
    grad_piece = halving_scatter(weight_terms, "dp")
    sum_first, sum_second = space_sum((local_first, local_second), "space")
    grad_piece = replicated_sum(grad_piece, "space")
    first = sum_first / cell_count
    second = sum_second / cell_count
    input_grad = (
        spread_groups(inverse, channels)
        * (scaled - spread_groups(first, channels) - normed * spread_groups(second, channels))
        * inside
    ).astype(jnp.bfloat16)
    first_new = 0.9 * moment_one + 0.1 * grad_piece
    second_new = 0.999 * moment_two + 0.001 * grad_piece * grad_piece
    adam_update = first_new / (1.0 - 0.9**10) / (jnp.sqrt(second_new / (1.0 - 0.999**10)) + 1e-08)
    return (block_out[None], input_grad[None], grad_piece, adam_update)


def solution(mesh):
    placed = (
        P("dp", "space", None, None),
        P("dp", "space", None, None),
        P(),
        P(),
        P("dp", None),
        P("dp", None),
        P("dp", None),
        P("dp"),
        P("dp"),
    )
    return jax.shard_map(
        local,
        mesh=mesh,
        in_specs=placed,
        out_specs=(
            P("dp", "space", None, None),
            P("dp", "space", None, None),
            P("dp", None),
            P("dp", None),
        ),
        check_vma=False,
    )
```

```python
import jax
import jax.numpy as jnp
from jax import lax
from jax.sharding import PartitionSpec as P

GROUPS = 32


def with_halo(cells, sides, width):
    for axis, dim in sides:
        count = lax.axis_size(axis)
        ends = count - 1
        head = lax.slice_in_dim(cells, 0, width, axis=dim)
        tail = lax.slice_in_dim(cells, cells.shape[dim] - width, cells.shape[dim], axis=dim)
        cells = jnp.concatenate(
            [
                lax.ppermute(tail, axis, [(i, (i + 1) % count) for i in range(ends)]),
                cells,
                lax.ppermute(head, axis, [((i + 1) % count, i) for i in range(ends)]),
            ],
            axis=dim,
        )
    return cells


def space_sum(parts, axis):
    count = lax.axis_size(axis)
    if count > 4:
        return lax.psum(parts, axis)
    joined = jnp.stack(parts)
    shifted = [
        lax.ppermute(joined, axis, [(i, (i + shift) % count) for i in range(count)])
        for shift in range(1, count)
    ]
    for got in shifted:
        joined = joined + got
    return tuple(joined)


def halving_scatter(partial, axis):
    count = lax.axis_size(axis)
    rows, channels = partial.shape[0] // count, partial.shape[1]
    if count & (count - 1):
        summed = lax.psum_scatter(
            partial.astype(jnp.bfloat16).reshape(count, rows, channels),
            axis,
            scatter_dimension=0,
            tiled=False,
        )
        return summed.astype(jnp.float32)
    index = lax.axis_index(axis)
    held = partial.reshape(count, rows, channels)
    step = 1
    while step < count:
        bit = (index // step) % 2
        paired = held.reshape(-1, 2, rows, channels)
        keep = lax.dynamic_index_in_dim(paired, bit, axis=1, keepdims=False)
        send = lax.dynamic_index_in_dim(paired, 1 - bit, axis=1, keepdims=False)
        pairs = [(i, i ^ step) for i in range(count)]
        got = lax.ppermute(send.astype(jnp.bfloat16), axis, pairs)
        held = keep + got.astype(jnp.float32)
        step *= 2
    return held[0]


def replicated_sum(value, axis):
    count = lax.axis_size(axis)
    if count & (count - 1):
        return lax.psum(value.astype(jnp.bfloat16), axis).astype(jnp.float32)
    step = 1
    while step < count:
        mine = value.astype(jnp.bfloat16)
        pairs = [(i, i ^ step) for i in range(count)]
        value = mine.astype(jnp.float32) + lax.ppermute(mine, axis, pairs).astype(jnp.float32)
        step *= 2
    return value


def group_sum(values, groups):
    height_dev, width_dev, channels = values.shape
    return values.reshape(height_dev, width_dev, groups, channels // groups).sum(axis=(0, 1, 3))


def spread_groups(statistic, channels):
    return jnp.repeat(statistic, channels // statistic.shape[0])


def pad_columns(padded_rows):
    return jnp.pad(padded_rows, ((0, 0), (1, 1), (0, 0)))


def local(
    features, cotangent, norm_gain, norm_bias, weight, moment_one, moment_two, heights, widths
):
    latent = features[0]
    height_dev, width_dev, channels = latent.shape
    row_ids = lax.axis_index("space") * height_dev + jnp.arange(height_dev, dtype=jnp.int32)
    inside = (
        (row_ids < heights[0])[:, None]
        & (jnp.arange(width_dev, dtype=jnp.int32) < widths[0])[None, :]
    ).astype(jnp.float32)[..., None]
    cell_count = (heights[0] * widths[0] * (channels // GROUPS)).astype(jnp.float32)
    gathered = lax.all_gather(weight, "dp", axis=0, tiled=True)
    values = latent.astype(jnp.float32) * inside
    group_total, squares = space_sum(
        (group_sum(values, GROUPS), group_sum(values * values, GROUPS)), "space"
    )
    center = group_total / cell_count
    spread = squares / cell_count - center * center
    inverse = lax.rsqrt(spread + 1e-05)
    normed = (values - spread_groups(center, channels)) * spread_groups(inverse, channels) * inside
    before = normed * norm_gain + norm_bias
    activated = (jax.nn.silu(before) * inside).astype(jnp.bfloat16)
    act_pad = pad_columns(with_halo(activated, (("space", 0),), 1))
    act_cols = jnp.concatenate(
        [
            act_pad[row_off : row_off + height_dev, col_off : col_off + width_dev]
            for row_off in range(3)
            for col_off in range(3)
        ],
        axis=-1,
    ).reshape(height_dev * width_dev, 9 * channels)
    masked = cotangent[0] * inside.astype(jnp.bfloat16)
    cot_pad = pad_columns(with_halo(masked, (("space", 0),), 1))
    flat_cot = masked.reshape(-1, channels)
    weight_terms = lax.dot_general(
        act_cols, flat_cot, (((0,), (0,)), ((), ())), preferred_element_type=jnp.float32
    )
    weight_terms, gathered, cot_pad = lax.optimization_barrier((weight_terms, gathered, cot_pad))
    output = jnp.dot(act_cols, gathered, preferred_element_type=jnp.float32)
    block_out = (output.reshape(height_dev, width_dev, channels) * inside).astype(jnp.bfloat16)
    tap_weights = gathered.reshape(9, channels, channels)
    cot_cols = jnp.concatenate(
        [
            cot_pad[2 - row_off : 2 - row_off + height_dev, 2 - col_off : 2 - col_off + width_dev]
            for row_off in range(3)
            for col_off in range(3)
        ],
        axis=-1,
    ).reshape(height_dev * width_dev, 9 * channels)
    flipped = tap_weights.transpose(0, 2, 1).reshape(9 * channels, channels)
    upstream = jnp.dot(cot_cols, flipped, preferred_element_type=jnp.float32)
    gate_sig = jax.nn.sigmoid(before)
    silu_slope = gate_sig * (1.0 + before * (1.0 - gate_sig))
    scaled = upstream.reshape(height_dev, width_dev, channels) * silu_slope * inside * norm_gain
    local_first = group_sum(scaled, GROUPS)
    local_second = group_sum(scaled * normed, GROUPS)
    grad_piece = halving_scatter(weight_terms, "dp")
    sum_first, sum_second = space_sum((local_first, local_second), "space")
    grad_piece = replicated_sum(grad_piece, "space")
    first = sum_first / cell_count
    second = sum_second / cell_count
    input_grad = (
        spread_groups(inverse, channels)
        * (scaled - spread_groups(first, channels) - normed * spread_groups(second, channels))
        * inside
    ).astype(jnp.bfloat16)
    first_new = 0.9 * moment_one + 0.1 * grad_piece
    second_new = 0.999 * moment_two + 0.001 * grad_piece * grad_piece
    adam_update = first_new / (1.0 - 0.9**10) / (jnp.sqrt(second_new / (1.0 - 0.999**10)) + 1e-08)
    return (block_out[None], input_grad[None], grad_piece, adam_update)


def solution(mesh):
    placed = (
        P("dp", "space", None, None),
        P("dp", "space", None, None),
        P(),
        P(),
        P("dp", None),
        P("dp", None),
        P("dp", None),
        P("dp"),
        P("dp"),
    )
    return jax.shard_map(
        local,
        mesh=mesh,
        in_specs=placed,
        out_specs=(
            P("dp", "space", None, None),
            P("dp", "space", None, None),
            P("dp", None),
            P("dp", None),
        ),
        check_vma=False,
    )
```

```python
import jax
import jax.numpy as jnp
from jax import lax
from jax.experimental.layout import Layout, with_layout_constraint
from jax.sharding import PartitionSpec as P

GROUPS = 32


def with_halo(cells, sides, width):
    for axis, dim in sides:
        count = lax.axis_size(axis)
        ends = count - 1
        head = lax.slice_in_dim(cells, 0, width, axis=dim)
        tail = lax.slice_in_dim(cells, cells.shape[dim] - width, cells.shape[dim], axis=dim)
        cells = jnp.concatenate(
            [
                lax.ppermute(tail, axis, [(i, (i + 1) % count) for i in range(ends)]),
                cells,
                lax.ppermute(head, axis, [((i + 1) % count, i) for i in range(ends)]),
            ],
            axis=dim,
        )
    return cells


def space_sum(parts, axis):
    count = lax.axis_size(axis)
    if count > 4:
        return lax.psum(parts, axis)
    joined = jnp.stack(parts)
    shifted = [
        lax.ppermute(joined, axis, [(i, (i + shift) % count) for i in range(count)])
        for shift in range(1, count)
    ]
    for got in shifted:
        joined = joined + got
    return tuple(joined)


def row_major(value):
    return with_layout_constraint(value, Layout(major_to_minor=tuple(range(value.ndim))))


def halving_scatter(partial, axis):
    count = lax.axis_size(axis)
    rows, channels = partial.shape[0] // count, partial.shape[1]
    if count & (count - 1):
        summed = lax.psum_scatter(
            partial.astype(jnp.bfloat16).reshape(count, rows, channels),
            axis,
            scatter_dimension=0,
            tiled=False,
        )
        return summed.astype(jnp.float32)
    index = lax.axis_index(axis)
    held = partial.reshape(count, rows, channels)
    step = 1
    while step < count:
        bit = (index // step) % 2
        paired = held.reshape(-1, 2, rows, channels)
        keep = row_major(lax.dynamic_index_in_dim(paired, bit, axis=1, keepdims=False))
        send = row_major(lax.dynamic_index_in_dim(paired, 1 - bit, axis=1, keepdims=False))
        pairs = [(i, i ^ step) for i in range(count)]
        got = lax.ppermute(send.astype(jnp.bfloat16), axis, pairs)
        held = row_major(keep + got.astype(jnp.float32))
        step *= 2
    return held[0]


def replicated_sum(value, axis):
    count = lax.axis_size(axis)
    if count & (count - 1):
        return lax.psum(value.astype(jnp.bfloat16), axis).astype(jnp.float32)
    step = 1
    while step < count:
        mine = value.astype(jnp.bfloat16)
        pairs = [(i, i ^ step) for i in range(count)]
        value = mine.astype(jnp.float32) + lax.ppermute(mine, axis, pairs).astype(jnp.float32)
        step *= 2
    return value


def group_sum(values, groups):
    height_dev, width_dev, channels = values.shape
    return values.reshape(height_dev, width_dev, groups, channels // groups).sum(axis=(0, 1, 3))


def spread_groups(statistic, channels):
    return jnp.repeat(statistic, channels // statistic.shape[0])


def pad_columns(padded_rows):
    return jnp.pad(padded_rows, ((0, 0), (1, 1), (0, 0)))


def local(
    features, cotangent, norm_gain, norm_bias, weight, moment_one, moment_two, heights, widths
):
    latent = features[0]
    height_dev, width_dev, channels = latent.shape
    row_ids = lax.axis_index("space") * height_dev + jnp.arange(height_dev, dtype=jnp.int32)
    inside = (
        (row_ids < heights[0])[:, None]
        & (jnp.arange(width_dev, dtype=jnp.int32) < widths[0])[None, :]
    ).astype(jnp.float32)[..., None]
    cell_count = (heights[0] * widths[0] * (channels // GROUPS)).astype(jnp.float32)
    gathered = lax.all_gather(weight, "dp", axis=0, tiled=True)
    values = latent.astype(jnp.float32) * inside
    group_total, squares = space_sum(
        (group_sum(values, GROUPS), group_sum(values * values, GROUPS)), "space"
    )
    center = group_total / cell_count
    spread = squares / cell_count - center * center
    inverse = lax.rsqrt(spread + 1e-05)
    normed = (values - spread_groups(center, channels)) * spread_groups(inverse, channels) * inside
    before = normed * norm_gain + norm_bias
    activated = (jax.nn.silu(before) * inside).astype(jnp.bfloat16)
    act_pad = pad_columns(with_halo(activated, (("space", 0),), 1))
    act_cols = jnp.concatenate(
        [
            act_pad[row_off : row_off + height_dev, col_off : col_off + width_dev]
            for row_off in range(3)
            for col_off in range(3)
        ],
        axis=-1,
    ).reshape(height_dev * width_dev, 9 * channels)
    masked = cotangent[0] * inside.astype(jnp.bfloat16)
    cot_pad = pad_columns(with_halo(masked, (("space", 0),), 1))
    flat_cot = masked.reshape(-1, channels)
    weight_terms = lax.dot_general(
        act_cols, flat_cot, (((0,), (0,)), ((), ())), preferred_element_type=jnp.float32
    )
    weight_terms = row_major(weight_terms)
    weight_terms, gathered, cot_pad = lax.optimization_barrier((weight_terms, gathered, cot_pad))
    output = jnp.dot(act_cols, gathered, preferred_element_type=jnp.float32)
    block_out = (output.reshape(height_dev, width_dev, channels) * inside).astype(jnp.bfloat16)
    tap_weights = gathered.reshape(9, channels, channels)
    cot_cols = jnp.concatenate(
        [
            cot_pad[2 - row_off : 2 - row_off + height_dev, 2 - col_off : 2 - col_off + width_dev]
            for row_off in range(3)
            for col_off in range(3)
        ],
        axis=-1,
    ).reshape(height_dev * width_dev, 9 * channels)
    flipped = tap_weights.transpose(0, 2, 1).reshape(9 * channels, channels)
    upstream = jnp.dot(cot_cols, flipped, preferred_element_type=jnp.float32)
    gate_sig = jax.nn.sigmoid(before)
    silu_slope = gate_sig * (1.0 + before * (1.0 - gate_sig))
    scaled = upstream.reshape(height_dev, width_dev, channels) * silu_slope * inside * norm_gain
    local_first = group_sum(scaled, GROUPS)
    local_second = group_sum(scaled * normed, GROUPS)
    grad_piece = halving_scatter(weight_terms, "dp")
    sum_first, sum_second = space_sum((local_first, local_second), "space")
    grad_piece = replicated_sum(grad_piece, "space")
    first = sum_first / cell_count
    second = sum_second / cell_count
    input_grad = (
        spread_groups(inverse, channels)
        * (scaled - spread_groups(first, channels) - normed * spread_groups(second, channels))
        * inside
    ).astype(jnp.bfloat16)
    first_new = 0.9 * moment_one + 0.1 * grad_piece
    second_new = 0.999 * moment_two + 0.001 * grad_piece * grad_piece
    adam_update = first_new / (1.0 - 0.9**10) / (jnp.sqrt(second_new / (1.0 - 0.999**10)) + 1e-08)
    return (block_out[None], input_grad[None], grad_piece, adam_update)


def solution(mesh):
    placed = (
        P("dp", "space", None, None),
        P("dp", "space", None, None),
        P(),
        P(),
        P("dp", None),
        P("dp", None),
        P("dp", None),
        P("dp"),
        P("dp"),
    )
    return jax.shard_map(
        local,
        mesh=mesh,
        in_specs=placed,
        out_specs=(
            P("dp", "space", None, None),
            P("dp", "space", None, None),
            P("dp", None),
            P("dp", None),
        ),
        check_vma=False,
    )
```

```python
import jax
import jax.numpy as jnp
from jax import lax
from jax.experimental.layout import Layout, with_layout_constraint
from jax.sharding import PartitionSpec as P

GROUPS = 32


def with_halo(cells, sides, width):
    for axis, dim in sides:
        count = lax.axis_size(axis)
        ends = count - 1
        head = lax.slice_in_dim(cells, 0, width, axis=dim)
        tail = lax.slice_in_dim(cells, cells.shape[dim] - width, cells.shape[dim], axis=dim)
        cells = jnp.concatenate(
            [
                lax.ppermute(tail, axis, [(i, (i + 1) % count) for i in range(ends)]),
                cells,
                lax.ppermute(head, axis, [((i + 1) % count, i) for i in range(ends)]),
            ],
            axis=dim,
        )
    return cells


def space_sum(parts, axis):
    count = lax.axis_size(axis)
    if count > 4:
        return lax.psum(parts, axis)
    joined = jnp.stack(parts)
    shifted = [
        lax.ppermute(joined, axis, [(i, (i + shift) % count) for i in range(count)])
        for shift in range(1, count)
    ]
    for got in shifted:
        joined = joined + got
    return tuple(joined)


def row_major(value):
    return with_layout_constraint(value, Layout(major_to_minor=tuple(range(value.ndim))))


def halving_scatter(partial, axis, companions):
    count = lax.axis_size(axis)
    rows, channels = partial.shape[0] // count, partial.shape[1]
    if count & (count - 1):
        summed = lax.psum_scatter(
            partial.astype(jnp.bfloat16).reshape(count, rows, channels),
            axis,
            scatter_dimension=0,
            tiled=False,
        )
        return summed.astype(jnp.float32), companions
    index = lax.axis_index(axis)
    held = partial.reshape(count, rows, channels)
    step = 1
    while step < count:
        bit = (index // step) % 2
        paired = held.reshape(-1, 2, rows, channels)
        keep = row_major(lax.dynamic_index_in_dim(paired, bit, axis=1, keepdims=False))
        send = row_major(lax.dynamic_index_in_dim(paired, 1 - bit, axis=1, keepdims=False))
        pairs = [(i, i ^ step) for i in range(count)]
        got = lax.ppermute(send.astype(jnp.bfloat16), axis, pairs)
        held = row_major(keep + got.astype(jnp.float32))
        if step == 1:
            held, companions = lax.optimization_barrier((held, companions))
        step *= 2
    return held[0], companions


def replicated_sum(value, axis):
    count = lax.axis_size(axis)
    if count & (count - 1):
        return lax.psum(value.astype(jnp.bfloat16), axis).astype(jnp.float32)
    step = 1
    while step < count:
        mine = value.astype(jnp.bfloat16)
        pairs = [(i, i ^ step) for i in range(count)]
        value = mine.astype(jnp.float32) + lax.ppermute(mine, axis, pairs).astype(jnp.float32)
        step *= 2
    return value


def group_sum(values, groups):
    height_dev, width_dev, channels = values.shape
    return values.reshape(height_dev, width_dev, groups, channels // groups).sum(axis=(0, 1, 3))


def spread_groups(statistic, channels):
    return jnp.repeat(statistic, channels // statistic.shape[0])


def pad_columns(padded_rows):
    return jnp.pad(padded_rows, ((0, 0), (1, 1), (0, 0)))


def local(
    features, cotangent, norm_gain, norm_bias, weight, moment_one, moment_two, heights, widths
):
    latent = features[0]
    height_dev, width_dev, channels = latent.shape
    row_ids = lax.axis_index("space") * height_dev + jnp.arange(height_dev, dtype=jnp.int32)
    inside = (
        (row_ids < heights[0])[:, None]
        & (jnp.arange(width_dev, dtype=jnp.int32) < widths[0])[None, :]
    ).astype(jnp.float32)[..., None]
    cell_count = (heights[0] * widths[0] * (channels // GROUPS)).astype(jnp.float32)
    gathered = row_major(lax.all_gather(row_major(weight), "dp", axis=0, tiled=True))
    values = latent.astype(jnp.float32) * inside
    group_total, squares = space_sum(
        (group_sum(values, GROUPS), group_sum(values * values, GROUPS)), "space"
    )
    center = group_total / cell_count
    spread = squares / cell_count - center * center
    inverse = lax.rsqrt(spread + 1e-05)
    normed = (values - spread_groups(center, channels)) * spread_groups(inverse, channels) * inside
    before = normed * norm_gain + norm_bias
    activated = (jax.nn.silu(before) * inside).astype(jnp.bfloat16)
    act_pad = pad_columns(with_halo(activated, (("space", 0),), 1))
    act_cols = jnp.concatenate(
        [
            act_pad[row_off : row_off + height_dev, col_off : col_off + width_dev]
            for row_off in range(3)
            for col_off in range(3)
        ],
        axis=-1,
    ).reshape(height_dev * width_dev, 9 * channels)
    masked = cotangent[0] * inside.astype(jnp.bfloat16)
    cot_pad = pad_columns(with_halo(masked, (("space", 0),), 1))
    flat_cot = masked.reshape(-1, channels)
    weight_terms = lax.dot_general(
        act_cols, flat_cot, (((0,), (0,)), ((), ())), preferred_element_type=jnp.float32
    )
    weight_terms = row_major(weight_terms)
    grad_piece, (gathered, cot_pad) = halving_scatter(weight_terms, "dp", (gathered, cot_pad))
    output = jnp.dot(act_cols, gathered, preferred_element_type=jnp.float32)
    block_out = (output.reshape(height_dev, width_dev, channels) * inside).astype(jnp.bfloat16)
    tap_weights = gathered.reshape(9, channels, channels)
    cot_cols = jnp.concatenate(
        [
            cot_pad[2 - row_off : 2 - row_off + height_dev, 2 - col_off : 2 - col_off + width_dev]
            for row_off in range(3)
            for col_off in range(3)
        ],
        axis=-1,
    ).reshape(height_dev * width_dev, 9 * channels)
    flipped = tap_weights.transpose(0, 2, 1).reshape(9 * channels, channels)
    upstream = jnp.dot(cot_cols, flipped, preferred_element_type=jnp.float32)
    gate_sig = jax.nn.sigmoid(before)
    silu_slope = gate_sig * (1.0 + before * (1.0 - gate_sig))
    scaled = upstream.reshape(height_dev, width_dev, channels) * silu_slope * inside * norm_gain
    local_first = group_sum(scaled, GROUPS)
    local_second = group_sum(scaled * normed, GROUPS)
    sum_first, sum_second = space_sum((local_first, local_second), "space")
    grad_piece = replicated_sum(grad_piece, "space")
    first = sum_first / cell_count
    second = sum_second / cell_count
    input_grad = (
        spread_groups(inverse, channels)
        * (scaled - spread_groups(first, channels) - normed * spread_groups(second, channels))
        * inside
    ).astype(jnp.bfloat16)
    first_new = 0.9 * moment_one + 0.1 * grad_piece
    second_new = 0.999 * moment_two + 0.001 * grad_piece * grad_piece
    adam_update = first_new / (1.0 - 0.9**10) / (jnp.sqrt(second_new / (1.0 - 0.999**10)) + 1e-08)
    return (block_out[None], input_grad[None], grad_piece, adam_update)


def solution(mesh):
    placed = (
        P("dp", "space", None, None),
        P("dp", "space", None, None),
        P(),
        P(),
        P("dp", None),
        P("dp", None),
        P("dp", None),
        P("dp"),
        P("dp"),
    )
    return jax.shard_map(
        local,
        mesh=mesh,
        in_specs=placed,
        out_specs=(
            P("dp", "space", None, None),
            P("dp", "space", None, None),
            P("dp", None),
            P("dp", None),
        ),
        check_vma=False,
    )
```

```python
import jax
import jax.numpy as jnp
from jax import lax
from jax.experimental.layout import Layout, with_layout_constraint
from jax.sharding import PartitionSpec as P

GROUPS = 32


def with_halo(cells, sides, width):
    for axis, dim in sides:
        count = lax.axis_size(axis)
        ends = count - 1
        head = lax.slice_in_dim(cells, 0, width, axis=dim)
        tail = lax.slice_in_dim(cells, cells.shape[dim] - width, cells.shape[dim], axis=dim)
        cells = jnp.concatenate(
            [
                lax.ppermute(tail, axis, [(i, (i + 1) % count) for i in range(ends)]),
                cells,
                lax.ppermute(head, axis, [((i + 1) % count, i) for i in range(ends)]),
            ],
            axis=dim,
        )
    return cells


def space_sum(parts, axis):
    count = lax.axis_size(axis)
    if count > 4:
        return lax.psum(parts, axis)
    joined = jnp.stack(parts)
    shifted = [
        lax.ppermute(joined, axis, [(i, (i + shift) % count) for i in range(count)])
        for shift in range(1, count)
    ]
    for got in shifted:
        joined = joined + got
    return tuple(joined)


def row_major(value):
    return with_layout_constraint(value, Layout(major_to_minor=tuple(range(value.ndim))))


def halving_scatter(partial, axis, companions):
    count = lax.axis_size(axis)
    rows, channels = partial.shape[0] // count, partial.shape[1]
    if count & (count - 1):
        summed = lax.psum_scatter(
            partial.astype(jnp.bfloat16).reshape(count, rows, channels),
            axis,
            scatter_dimension=0,
            tiled=False,
        )
        return summed.astype(jnp.float32), companions
    index = lax.axis_index(axis)
    held = partial.reshape(count, rows, channels)
    step = 1
    while step < count:
        bit = (index // step) % 2
        paired = held.reshape(-1, 2, rows, channels)
        keep = row_major(lax.dynamic_index_in_dim(paired, bit, axis=1, keepdims=False))
        send = row_major(lax.dynamic_index_in_dim(paired, 1 - bit, axis=1, keepdims=False))
        pairs = [(i, i ^ step) for i in range(count)]
        got = lax.ppermute(send.astype(jnp.bfloat16), axis, pairs)
        held = row_major(keep + got.astype(jnp.float32))
        if step == 1:
            held, companions = lax.optimization_barrier((held, companions))
        step *= 2
        if step < count <= 4 * step:
            break
    if step == count:
        return held[0], companions
    spots = count // step
    own = index // step
    total = lax.dynamic_index_in_dim(held, own, keepdims=False)
    for shift in range(1, spots):
        send = lax.dynamic_index_in_dim(held, own ^ shift, keepdims=False)
        pairs = [(i, i ^ (shift * step)) for i in range(count)]
        total = total + lax.ppermute(send.astype(jnp.bfloat16), axis, pairs).astype(jnp.float32)
    return total, companions


def replicated_sum(value, axis):
    count = lax.axis_size(axis)
    if count & (count - 1):
        return lax.psum(value.astype(jnp.bfloat16), axis).astype(jnp.float32)
    step = 1
    while step < count:
        mine = value.astype(jnp.bfloat16)
        pairs = [(i, i ^ step) for i in range(count)]
        value = mine.astype(jnp.float32) + lax.ppermute(mine, axis, pairs).astype(jnp.float32)
        step *= 2
    return value


def group_sum(values, groups):
    height_dev, width_dev, channels = values.shape
    return values.reshape(height_dev, width_dev, groups, channels // groups).sum(axis=(0, 1, 3))


def spread_groups(statistic, channels):
    return jnp.repeat(statistic, channels // statistic.shape[0])


def pad_columns(padded_rows):
    return jnp.pad(padded_rows, ((0, 0), (1, 1), (0, 0)))


def local(
    features, cotangent, norm_gain, norm_bias, weight, moment_one, moment_two, heights, widths
):
    latent = features[0]
    height_dev, width_dev, channels = latent.shape
    row_ids = lax.axis_index("space") * height_dev + jnp.arange(height_dev, dtype=jnp.int32)
    inside = (
        (row_ids < heights[0])[:, None]
        & (jnp.arange(width_dev, dtype=jnp.int32) < widths[0])[None, :]
    ).astype(jnp.float32)[..., None]
    cell_count = (heights[0] * widths[0] * (channels // GROUPS)).astype(jnp.float32)
    gathered = row_major(lax.all_gather(row_major(weight), "dp", axis=0, tiled=True))
    values = latent.astype(jnp.float32) * inside
    group_total, squares = space_sum(
        (group_sum(values, GROUPS), group_sum(values * values, GROUPS)), "space"
    )
    center = group_total / cell_count
    spread = squares / cell_count - center * center
    inverse = lax.rsqrt(spread + 1e-05)
    normed = (values - spread_groups(center, channels)) * spread_groups(inverse, channels) * inside
    before = normed * norm_gain + norm_bias
    activated = (jax.nn.silu(before) * inside).astype(jnp.bfloat16)
    act_pad = pad_columns(with_halo(activated, (("space", 0),), 1))
    act_cols = jnp.concatenate(
        [
            act_pad[row_off : row_off + height_dev, col_off : col_off + width_dev]
            for row_off in range(3)
            for col_off in range(3)
        ],
        axis=-1,
    ).reshape(height_dev * width_dev, 9 * channels)
    masked = cotangent[0] * inside.astype(jnp.bfloat16)
    cot_pad = pad_columns(with_halo(masked, (("space", 0),), 1))
    flat_cot = masked.reshape(-1, channels)
    weight_terms = lax.dot_general(
        act_cols, flat_cot, (((0,), (0,)), ((), ())), preferred_element_type=jnp.float32
    )
    weight_terms = row_major(weight_terms)
    grad_piece, (gathered, cot_pad) = halving_scatter(weight_terms, "dp", (gathered, cot_pad))
    output = jnp.dot(act_cols, gathered, preferred_element_type=jnp.float32)
    block_out = (output.reshape(height_dev, width_dev, channels) * inside).astype(jnp.bfloat16)
    tap_weights = gathered.reshape(9, channels, channels)
    cot_cols = jnp.concatenate(
        [
            cot_pad[2 - row_off : 2 - row_off + height_dev, 2 - col_off : 2 - col_off + width_dev]
            for row_off in range(3)
            for col_off in range(3)
        ],
        axis=-1,
    ).reshape(height_dev * width_dev, 9 * channels)
    flipped = tap_weights.transpose(0, 2, 1).reshape(9 * channels, channels)
    upstream = jnp.dot(cot_cols, flipped, preferred_element_type=jnp.float32)
    gate_sig = jax.nn.sigmoid(before)
    silu_slope = gate_sig * (1.0 + before * (1.0 - gate_sig))
    scaled = upstream.reshape(height_dev, width_dev, channels) * silu_slope * inside * norm_gain
    local_first = group_sum(scaled, GROUPS)
    local_second = group_sum(scaled * normed, GROUPS)
    sum_first, sum_second = space_sum((local_first, local_second), "space")
    grad_piece = with_layout_constraint(
        replicated_sum(grad_piece, "space"), Layout(major_to_minor=(1, 0))
    )
    first = sum_first / cell_count
    second = sum_second / cell_count
    input_grad = (
        spread_groups(inverse, channels)
        * (scaled - spread_groups(first, channels) - normed * spread_groups(second, channels))
        * inside
    ).astype(jnp.bfloat16)
    first_new = 0.9 * moment_one + 0.1 * grad_piece
    second_new = 0.999 * moment_two + 0.001 * grad_piece * grad_piece
    adam_update = first_new / (1.0 - 0.9**10) / (jnp.sqrt(second_new / (1.0 - 0.999**10)) + 1e-08)
    return (block_out[None], input_grad[None], grad_piece, adam_update)


def solution(mesh):
    placed = (
        P("dp", "space", None, None),
        P("dp", "space", None, None),
        P(),
        P(),
        P("dp", None),
        P("dp", None),
        P("dp", None),
        P("dp"),
        P("dp"),
    )
    return jax.shard_map(
        local,
        mesh=mesh,
        in_specs=placed,
        out_specs=(
            P("dp", "space", None, None),
            P("dp", "space", None, None),
            P("dp", None),
            P("dp", None),
        ),
        check_vma=False,
    )
```

```python
import jax
import jax.numpy as jnp
from jax import lax
from jax.experimental.layout import Layout, with_layout_constraint
from jax.sharding import PartitionSpec as P

GROUPS = 32


def with_halo(cells, sides, width):
    for axis, dim in sides:
        count = lax.axis_size(axis)
        ends = count - 1
        head = lax.slice_in_dim(cells, 0, width, axis=dim)
        tail = lax.slice_in_dim(cells, cells.shape[dim] - width, cells.shape[dim], axis=dim)
        cells = jnp.concatenate(
            [
                lax.ppermute(tail, axis, [(i, (i + 1) % count) for i in range(ends)]),
                cells,
                lax.ppermute(head, axis, [((i + 1) % count, i) for i in range(ends)]),
            ],
            axis=dim,
        )
    return cells


def space_sum(parts, axis):
    count = lax.axis_size(axis)
    if count > 4:
        return lax.psum(parts, axis)
    joined = jnp.stack(parts)
    shifted = [
        lax.ppermute(joined, axis, [(i, (i + shift) % count) for i in range(count)])
        for shift in range(1, count)
    ]
    for got in shifted:
        joined = joined + got
    return tuple(joined)


def row_major(value):
    return with_layout_constraint(value, Layout(major_to_minor=tuple(range(value.ndim))))


def halving_scatter(partial, axis, companions):
    count = lax.axis_size(axis)
    rows, channels = partial.shape[0] // count, partial.shape[1]
    if count & (count - 1):
        summed = lax.psum_scatter(
            partial.astype(jnp.bfloat16).reshape(count, rows, channels),
            axis,
            scatter_dimension=0,
            tiled=False,
        )
        return summed.astype(jnp.float32), companions
    index = lax.axis_index(axis)
    held = partial.reshape(count, rows, channels)
    step = 1
    while step < count:
        bit = (index // step) % 2
        paired = held.reshape(-1, 2, rows, channels)
        keep = row_major(lax.dynamic_index_in_dim(paired, bit, axis=1, keepdims=False))
        send = row_major(lax.dynamic_index_in_dim(paired, 1 - bit, axis=1, keepdims=False))
        pairs = [(i, i ^ step) for i in range(count)]
        got = lax.ppermute(send.astype(jnp.bfloat16), axis, pairs)
        held = row_major(keep + got.astype(jnp.float32))
        step *= 2
        if step < count <= 4 * step:
            break
    if step == count:
        return lax.optimization_barrier((held[0], companions))
    spots = count // step
    own = index // step
    total = lax.dynamic_index_in_dim(held, own, keepdims=False)
    for shift in range(1, spots):
        send = lax.dynamic_index_in_dim(held, own ^ shift, keepdims=False)
        pairs = [(i, i ^ (shift * step)) for i in range(count)]
        total = total + lax.ppermute(send.astype(jnp.bfloat16), axis, pairs).astype(jnp.float32)
    return lax.optimization_barrier((total, companions))


def replicated_sum(value, axis):
    count = lax.axis_size(axis)
    if count & (count - 1):
        return lax.psum(value.astype(jnp.bfloat16), axis).astype(jnp.float32)
    step = 1
    while step < count:
        mine = value.astype(jnp.bfloat16)
        pairs = [(i, i ^ step) for i in range(count)]
        value = mine.astype(jnp.float32) + lax.ppermute(mine, axis, pairs).astype(jnp.float32)
        step *= 2
    return value


def group_sum(values, groups):
    height_dev, width_dev, channels = values.shape
    return values.reshape(height_dev, width_dev, groups, channels // groups).sum(axis=(0, 1, 3))


def spread_groups(statistic, channels):
    return jnp.repeat(statistic, channels // statistic.shape[0])


def pad_columns(padded_rows):
    return jnp.pad(padded_rows, ((0, 0), (1, 1), (0, 0)))


def local(
    features, cotangent, norm_gain, norm_bias, weight, moment_one, moment_two, heights, widths
):
    latent = features[0]
    height_dev, width_dev, channels = latent.shape
    row_ids = lax.axis_index("space") * height_dev + jnp.arange(height_dev, dtype=jnp.int32)
    inside = (
        (row_ids < heights[0])[:, None]
        & (jnp.arange(width_dev, dtype=jnp.int32) < widths[0])[None, :]
    ).astype(jnp.float32)[..., None]
    cell_count = (heights[0] * widths[0] * (channels // GROUPS)).astype(jnp.float32)
    gathered = row_major(lax.all_gather(row_major(weight), "dp", axis=0, tiled=True))
    values = latent.astype(jnp.float32) * inside
    group_total, squares = space_sum(
        (group_sum(values, GROUPS), group_sum(values * values, GROUPS)), "space"
    )
    center = group_total / cell_count
    spread = squares / cell_count - center * center
    inverse = lax.rsqrt(spread + 1e-05)
    normed = (values - spread_groups(center, channels)) * spread_groups(inverse, channels) * inside
    before = normed * norm_gain + norm_bias
    activated = (jax.nn.silu(before) * inside).astype(jnp.bfloat16)
    act_pad = pad_columns(with_halo(activated, (("space", 0),), 1))
    act_cols = jnp.concatenate(
        [
            act_pad[row_off : row_off + height_dev, col_off : col_off + width_dev]
            for row_off in range(3)
            for col_off in range(3)
        ],
        axis=-1,
    ).reshape(height_dev * width_dev, 9 * channels)
    masked = cotangent[0] * inside.astype(jnp.bfloat16)
    cot_pad = pad_columns(with_halo(masked, (("space", 0),), 1))
    flat_cot = masked.reshape(-1, channels)
    weight_terms = lax.dot_general(
        act_cols, flat_cot, (((0,), (0,)), ((), ())), preferred_element_type=jnp.float32
    )
    weight_terms = row_major(weight_terms)
    grad_piece, (gathered, cot_pad) = halving_scatter(weight_terms, "dp", (gathered, cot_pad))
    output = jnp.dot(act_cols, gathered, preferred_element_type=jnp.float32)
    block_out = (output.reshape(height_dev, width_dev, channels) * inside).astype(jnp.bfloat16)
    tap_weights = gathered.reshape(9, channels, channels)
    cot_cols = jnp.concatenate(
        [
            cot_pad[2 - row_off : 2 - row_off + height_dev, 2 - col_off : 2 - col_off + width_dev]
            for row_off in range(3)
            for col_off in range(3)
        ],
        axis=-1,
    ).reshape(height_dev * width_dev, 9 * channels)
    flipped = tap_weights.transpose(0, 2, 1).reshape(9 * channels, channels)
    upstream = jnp.dot(cot_cols, flipped, preferred_element_type=jnp.float32)
    gate_sig = jax.nn.sigmoid(before)
    silu_slope = gate_sig * (1.0 + before * (1.0 - gate_sig))
    scaled = upstream.reshape(height_dev, width_dev, channels) * silu_slope * inside * norm_gain
    local_first = group_sum(scaled, GROUPS)
    local_second = group_sum(scaled * normed, GROUPS)
    sum_first, sum_second = space_sum((local_first, local_second), "space")
    grad_piece = with_layout_constraint(
        replicated_sum(grad_piece, "space"), Layout(major_to_minor=(1, 0))
    )
    first = sum_first / cell_count
    second = sum_second / cell_count
    input_grad = (
        spread_groups(inverse, channels)
        * (scaled - spread_groups(first, channels) - normed * spread_groups(second, channels))
        * inside
    ).astype(jnp.bfloat16)
    first_new = 0.9 * moment_one + 0.1 * grad_piece
    second_new = 0.999 * moment_two + 0.001 * grad_piece * grad_piece
    adam_update = first_new / (1.0 - 0.9**10) / (jnp.sqrt(second_new / (1.0 - 0.999**10)) + 1e-08)
    return (block_out[None], input_grad[None], grad_piece, adam_update)


def solution(mesh):
    placed = (
        P("dp", "space", None, None),
        P("dp", "space", None, None),
        P(),
        P(),
        P("dp", None),
        P("dp", None),
        P("dp", None),
        P("dp"),
        P("dp"),
    )
    return jax.shard_map(
        local,
        mesh=mesh,
        in_specs=placed,
        out_specs=(
            P("dp", "space", None, None),
            P("dp", "space", None, None),
            P("dp", None),
            P("dp", None),
        ),
        check_vma=False,
    )
```

```python
import jax
import jax.numpy as jnp
from jax import lax
from jax.experimental.layout import Layout, with_layout_constraint
from jax.sharding import PartitionSpec as P

GROUPS = 32


def with_halo(cells, sides, width):
    for axis, dim in sides:
        count = lax.axis_size(axis)
        ends = count - 1
        head = lax.slice_in_dim(cells, 0, width, axis=dim)
        tail = lax.slice_in_dim(cells, cells.shape[dim] - width, cells.shape[dim], axis=dim)
        cells = jnp.concatenate(
            [
                lax.ppermute(tail, axis, [(i, (i + 1) % count) for i in range(ends)]),
                cells,
                lax.ppermute(head, axis, [((i + 1) % count, i) for i in range(ends)]),
            ],
            axis=dim,
        )
    return cells


def space_sum(parts, axis):
    count = lax.axis_size(axis)
    if count > 4:
        return lax.psum(parts, axis)
    joined = jnp.stack(parts)
    shifted = [
        lax.ppermute(joined, axis, [(i, (i + shift) % count) for i in range(count)])
        for shift in range(1, count)
    ]
    for got in shifted:
        joined = joined + got
    return tuple(joined)


def row_major(value):
    return with_layout_constraint(value, Layout(major_to_minor=tuple(range(value.ndim))))


def halving_scatter(partial, axis, companions):
    count = lax.axis_size(axis)
    rows, channels = partial.shape[0] // count, partial.shape[1]
    if count & (count - 1):
        summed = lax.psum_scatter(
            partial.astype(jnp.bfloat16).reshape(count, rows, channels),
            axis,
            scatter_dimension=0,
            tiled=False,
        )
        return summed.astype(jnp.float32), companions
    index = lax.axis_index(axis)
    held = partial.reshape(count, rows, channels)
    step = 1
    while step < count:
        bit = (index // step) % 2
        paired = held.reshape(-1, 2, rows, channels)
        keep = row_major(lax.dynamic_index_in_dim(paired, bit, axis=1, keepdims=False))
        send = row_major(lax.dynamic_index_in_dim(paired, 1 - bit, axis=1, keepdims=False))
        pairs = [(i, i ^ step) for i in range(count)]
        got = lax.ppermute(send.astype(jnp.bfloat16), axis, pairs)
        held = row_major(keep + got.astype(jnp.float32))
        step *= 2
        if step < count <= 4 * step:
            break
    if step == count:
        return held[0], companions
    spots = count // step
    own = index // step
    total = lax.dynamic_index_in_dim(held, own, keepdims=False)
    for shift in range(1, spots):
        send = lax.dynamic_index_in_dim(held, own ^ shift, keepdims=False)
        pairs = [(i, i ^ (shift * step)) for i in range(count)]
        total = total + lax.ppermute(send.astype(jnp.bfloat16), axis, pairs).astype(jnp.float32)
    return total, companions


def replicated_sum(value, axis, companions):
    count = lax.axis_size(axis)
    if count & (count - 1):
        value, companions = lax.optimization_barrier((value, companions))
        return lax.psum(value.astype(jnp.bfloat16), axis).astype(jnp.float32), companions
    step = 1
    while step < count:
        mine = value.astype(jnp.bfloat16)
        pairs = [(i, i ^ step) for i in range(count)]
        value = mine.astype(jnp.float32) + lax.ppermute(mine, axis, pairs).astype(jnp.float32)
        if step == 1:
            value, companions = lax.optimization_barrier((value, companions))
        step *= 2
    return value, companions


def group_sum(values, groups):
    height_dev, width_dev, channels = values.shape
    return values.reshape(height_dev, width_dev, groups, channels // groups).sum(axis=(0, 1, 3))


def spread_groups(statistic, channels):
    return jnp.repeat(statistic, channels // statistic.shape[0])


def pad_columns(padded_rows):
    return jnp.pad(padded_rows, ((0, 0), (1, 1), (0, 0)))


def local(
    features, cotangent, norm_gain, norm_bias, weight, moment_one, moment_two, heights, widths
):
    latent = features[0]
    height_dev, width_dev, channels = latent.shape
    row_ids = lax.axis_index("space") * height_dev + jnp.arange(height_dev, dtype=jnp.int32)
    inside = (
        (row_ids < heights[0])[:, None]
        & (jnp.arange(width_dev, dtype=jnp.int32) < widths[0])[None, :]
    ).astype(jnp.float32)[..., None]
    cell_count = (heights[0] * widths[0] * (channels // GROUPS)).astype(jnp.float32)
    gathered = row_major(lax.all_gather(row_major(weight), "dp", axis=0, tiled=True))
    values = latent.astype(jnp.float32) * inside
    group_total, squares = space_sum(
        (group_sum(values, GROUPS), group_sum(values * values, GROUPS)), "space"
    )
    center = group_total / cell_count
    spread = squares / cell_count - center * center
    inverse = lax.rsqrt(spread + 1e-05)
    normed = (values - spread_groups(center, channels)) * spread_groups(inverse, channels) * inside
    before = normed * norm_gain + norm_bias
    activated = (jax.nn.silu(before) * inside).astype(jnp.bfloat16)
    act_pad = pad_columns(with_halo(activated, (("space", 0),), 1))
    act_cols = jnp.concatenate(
        [
            act_pad[row_off : row_off + height_dev, col_off : col_off + width_dev]
            for row_off in range(3)
            for col_off in range(3)
        ],
        axis=-1,
    ).reshape(height_dev * width_dev, 9 * channels)
    masked = cotangent[0] * inside.astype(jnp.bfloat16)
    cot_pad = pad_columns(with_halo(masked, (("space", 0),), 1))
    flat_cot = masked.reshape(-1, channels)
    weight_terms = lax.dot_general(
        act_cols, flat_cot, (((0,), (0,)), ((), ())), preferred_element_type=jnp.float32
    )
    weight_terms = row_major(weight_terms)
    grad_piece, companions = halving_scatter(weight_terms, "dp", (gathered, cot_pad))
    grad_piece, (gathered, cot_pad) = replicated_sum(grad_piece, "space", companions)
    output = jnp.dot(act_cols, gathered, preferred_element_type=jnp.float32)
    block_out = (output.reshape(height_dev, width_dev, channels) * inside).astype(jnp.bfloat16)
    tap_weights = gathered.reshape(9, channels, channels)
    cot_cols = jnp.concatenate(
        [
            cot_pad[2 - row_off : 2 - row_off + height_dev, 2 - col_off : 2 - col_off + width_dev]
            for row_off in range(3)
            for col_off in range(3)
        ],
        axis=-1,
    ).reshape(height_dev * width_dev, 9 * channels)
    flipped = tap_weights.transpose(0, 2, 1).reshape(9 * channels, channels)
    upstream = jnp.dot(cot_cols, flipped, preferred_element_type=jnp.float32)
    gate_sig = jax.nn.sigmoid(before)
    silu_slope = gate_sig * (1.0 + before * (1.0 - gate_sig))
    scaled = upstream.reshape(height_dev, width_dev, channels) * silu_slope * inside * norm_gain
    local_first = group_sum(scaled, GROUPS)
    local_second = group_sum(scaled * normed, GROUPS)
    sum_first, sum_second = space_sum((local_first, local_second), "space")
    grad_piece = with_layout_constraint(grad_piece, Layout(major_to_minor=(1, 0)))
    first = sum_first / cell_count
    second = sum_second / cell_count
    input_grad = (
        spread_groups(inverse, channels)
        * (scaled - spread_groups(first, channels) - normed * spread_groups(second, channels))
        * inside
    ).astype(jnp.bfloat16)
    first_new = 0.9 * moment_one + 0.1 * grad_piece
    second_new = 0.999 * moment_two + 0.001 * grad_piece * grad_piece
    adam_update = first_new / (1.0 - 0.9**10) / (jnp.sqrt(second_new / (1.0 - 0.999**10)) + 1e-08)
    return (block_out[None], input_grad[None], grad_piece, adam_update)


def solution(mesh):
    placed = (
        P("dp", "space", None, None),
        P("dp", "space", None, None),
        P(),
        P(),
        P("dp", None),
        P("dp", None),
        P("dp", None),
        P("dp"),
        P("dp"),
    )
    return jax.shard_map(
        local,
        mesh=mesh,
        in_specs=placed,
        out_specs=(
            P("dp", "space", None, None),
            P("dp", "space", None, None),
            P("dp", None),
            P("dp", None),
        ),
        check_vma=False,
    )
```

```python
import jax
import jax.numpy as jnp
from jax import lax
from jax.experimental.layout import Layout, with_layout_constraint
from jax.sharding import PartitionSpec as P

GROUPS = 32


def with_halo(cells, sides, width):
    for axis, dim in sides:
        count = lax.axis_size(axis)
        ends = count - 1
        head = lax.slice_in_dim(cells, 0, width, axis=dim)
        tail = lax.slice_in_dim(cells, cells.shape[dim] - width, cells.shape[dim], axis=dim)
        cells = jnp.concatenate(
            [
                lax.ppermute(tail, axis, [(i, (i + 1) % count) for i in range(ends)]),
                cells,
                lax.ppermute(head, axis, [((i + 1) % count, i) for i in range(ends)]),
            ],
            axis=dim,
        )
    return cells


def space_sum(parts, axis):
    count = lax.axis_size(axis)
    if count > 4:
        return lax.psum(parts, axis)
    joined = jnp.stack(parts)
    shifted = [
        lax.ppermute(joined, axis, [(i, (i + shift) % count) for i in range(count)])
        for shift in range(1, count)
    ]
    for got in shifted:
        joined = joined + got
    return tuple(joined)


def row_major(value):
    return with_layout_constraint(value, Layout(major_to_minor=tuple(range(value.ndim))))


def halving_scatter(partial, axis, companions):
    count = lax.axis_size(axis)
    rows, channels = partial.shape[0] // count, partial.shape[1]
    if count & (count - 1):
        summed = lax.psum_scatter(
            partial.astype(jnp.bfloat16).reshape(count, rows, channels),
            axis,
            scatter_dimension=0,
            tiled=False,
        )
        return summed.astype(jnp.float32), companions
    index = lax.axis_index(axis)
    held = partial.reshape(count, rows, channels)
    step = 1
    while step < count:
        bit = (index // step) % 2
        paired = held.reshape(-1, 2, rows, channels)
        keep = row_major(lax.dynamic_index_in_dim(paired, bit, axis=1, keepdims=False))
        send = row_major(lax.dynamic_index_in_dim(paired, 1 - bit, axis=1, keepdims=False))
        pairs = [(i, i ^ step) for i in range(count)]
        got = lax.ppermute(send.astype(jnp.bfloat16), axis, pairs)
        held = row_major(keep + got.astype(jnp.float32))
        if step == 1:
            held, companions = lax.optimization_barrier((held, companions))
        step *= 2
        if step < count <= 4 * step:
            break
    if step == count:
        return held[0], companions
    spots = count // step
    own = index // step
    total = lax.dynamic_index_in_dim(held, own, keepdims=False)
    for shift in range(1, spots):
        send = lax.dynamic_index_in_dim(held, own ^ shift, keepdims=False)
        pairs = [(i, i ^ (shift * step)) for i in range(count)]
        total = total + lax.ppermute(send.astype(jnp.bfloat16), axis, pairs).astype(jnp.float32)
    return total, companions


def replicated_sum(value, axis, companions):
    count = lax.axis_size(axis)
    if count & (count - 1):
        value, companions = lax.optimization_barrier((value, companions))
        return lax.psum(value.astype(jnp.bfloat16), axis).astype(jnp.float32), companions
    step = 1
    while step < count:
        mine = value.astype(jnp.bfloat16)
        pairs = [(i, i ^ step) for i in range(count)]
        value = mine.astype(jnp.float32) + lax.ppermute(mine, axis, pairs).astype(jnp.float32)
        if step == 1:
            value, companions = lax.optimization_barrier((value, companions))
        step *= 2
    return value, companions


def group_sum(values, groups):
    height_dev, width_dev, channels = values.shape
    return values.reshape(height_dev, width_dev, groups, channels // groups).sum(axis=(0, 1, 3))


def spread_groups(statistic, channels):
    return jnp.repeat(statistic, channels // statistic.shape[0])


def pad_columns(padded_rows):
    return jnp.pad(padded_rows, ((0, 0), (1, 1), (0, 0)))


def local(
    features, cotangent, norm_gain, norm_bias, weight, moment_one, moment_two, heights, widths
):
    latent = features[0]
    height_dev, width_dev, channels = latent.shape
    row_ids = lax.axis_index("space") * height_dev + jnp.arange(height_dev, dtype=jnp.int32)
    inside = (
        (row_ids < heights[0])[:, None]
        & (jnp.arange(width_dev, dtype=jnp.int32) < widths[0])[None, :]
    ).astype(jnp.float32)[..., None]
    cell_count = (heights[0] * widths[0] * (channels // GROUPS)).astype(jnp.float32)
    gathered = row_major(lax.all_gather(row_major(weight), "dp", axis=0, tiled=True))
    values = latent.astype(jnp.float32) * inside
    group_total, squares = space_sum(
        (group_sum(values, GROUPS), group_sum(values * values, GROUPS)), "space"
    )
    center = group_total / cell_count
    spread = squares / cell_count - center * center
    inverse = lax.rsqrt(spread + 1e-05)
    normed = (values - spread_groups(center, channels)) * spread_groups(inverse, channels) * inside
    before = normed * norm_gain + norm_bias
    activated = (jax.nn.silu(before) * inside).astype(jnp.bfloat16)
    act_pad = pad_columns(with_halo(activated, (("space", 0),), 1))
    act_cols = jnp.concatenate(
        [
            act_pad[row_off : row_off + height_dev, col_off : col_off + width_dev]
            for row_off in range(3)
            for col_off in range(3)
        ],
        axis=-1,
    ).reshape(height_dev * width_dev, 9 * channels)
    masked = cotangent[0] * inside.astype(jnp.bfloat16)
    cot_pad = pad_columns(with_halo(masked, (("space", 0),), 1))
    flat_cot = masked.reshape(-1, channels)
    weight_terms = lax.dot_general(
        act_cols, flat_cot, (((0,), (0,)), ((), ())), preferred_element_type=jnp.float32
    )
    weight_terms = row_major(weight_terms)
    grad_piece, gathered = halving_scatter(weight_terms, "dp", gathered)
    grad_piece, (gathered, cot_pad) = replicated_sum(grad_piece, "space", (gathered, cot_pad))
    output = jnp.dot(act_cols, gathered, preferred_element_type=jnp.float32)
    block_out = (output.reshape(height_dev, width_dev, channels) * inside).astype(jnp.bfloat16)
    tap_weights = gathered.reshape(9, channels, channels)
    cot_cols = jnp.concatenate(
        [
            cot_pad[2 - row_off : 2 - row_off + height_dev, 2 - col_off : 2 - col_off + width_dev]
            for row_off in range(3)
            for col_off in range(3)
        ],
        axis=-1,
    ).reshape(height_dev * width_dev, 9 * channels)
    flipped = tap_weights.transpose(0, 2, 1).reshape(9 * channels, channels)
    upstream = jnp.dot(cot_cols, flipped, preferred_element_type=jnp.float32)
    gate_sig = jax.nn.sigmoid(before)
    silu_slope = gate_sig * (1.0 + before * (1.0 - gate_sig))
    scaled = upstream.reshape(height_dev, width_dev, channels) * silu_slope * inside * norm_gain
    local_first = group_sum(scaled, GROUPS)
    local_second = group_sum(scaled * normed, GROUPS)
    sum_first, sum_second = space_sum((local_first, local_second), "space")
    grad_piece = with_layout_constraint(grad_piece, Layout(major_to_minor=(1, 0)))
    first = sum_first / cell_count
    second = sum_second / cell_count
    input_grad = (
        spread_groups(inverse, channels)
        * (scaled - spread_groups(first, channels) - normed * spread_groups(second, channels))
        * inside
    ).astype(jnp.bfloat16)
    first_new = 0.9 * moment_one + 0.1 * grad_piece
    second_new = 0.999 * moment_two + 0.001 * grad_piece * grad_piece
    adam_update = first_new / (1.0 - 0.9**10) / (jnp.sqrt(second_new / (1.0 - 0.999**10)) + 1e-08)
    return (block_out[None], input_grad[None], grad_piece, adam_update)


def solution(mesh):
    placed = (
        P("dp", "space", None, None),
        P("dp", "space", None, None),
        P(),
        P(),
        P("dp", None),
        P("dp", None),
        P("dp", None),
        P("dp"),
        P("dp"),
    )
    return jax.shard_map(
        local,
        mesh=mesh,
        in_specs=placed,
        out_specs=(
            P("dp", "space", None, None),
            P("dp", "space", None, None),
            P("dp", None),
            P("dp", None),
        ),
        check_vma=False,
    )
```

```python
import jax
import jax.numpy as jnp
from jax import lax
from jax.experimental.layout import Layout, with_layout_constraint
from jax.sharding import PartitionSpec as P

GROUPS = 32


def with_halo(cells, sides, width):
    for axis, dim in sides:
        count = lax.axis_size(axis)
        ends = count - 1
        head = lax.slice_in_dim(cells, 0, width, axis=dim)
        tail = lax.slice_in_dim(cells, cells.shape[dim] - width, cells.shape[dim], axis=dim)
        cells = jnp.concatenate(
            [
                lax.ppermute(tail, axis, [(i, (i + 1) % count) for i in range(ends)]),
                cells,
                lax.ppermute(head, axis, [((i + 1) % count, i) for i in range(ends)]),
            ],
            axis=dim,
        )
    return cells


def space_sum(parts, axis):
    count = lax.axis_size(axis)
    if count > 4:
        return lax.psum(parts, axis)
    joined = jnp.stack(parts)
    shifted = [
        lax.ppermute(joined, axis, [(i, (i + shift) % count) for i in range(count)])
        for shift in range(1, count)
    ]
    for got in shifted:
        joined = joined + got
    return tuple(joined)


def row_major(value):
    return with_layout_constraint(value, Layout(major_to_minor=tuple(range(value.ndim))))


def halving_scatter(partial, axis, companions):
    count = lax.axis_size(axis)
    rows, channels = partial.shape[0] // count, partial.shape[1]
    if count & (count - 1):
        summed = lax.psum_scatter(
            partial.astype(jnp.bfloat16).reshape(count, rows, channels),
            axis,
            scatter_dimension=0,
            tiled=False,
        )
        return summed.astype(jnp.float32), companions
    index = lax.axis_index(axis)
    held = partial.reshape(count, rows, channels)
    step = 1
    while step < count:
        bit = (index // step) % 2
        paired = held.reshape(-1, 2, rows, channels)
        keep = row_major(lax.dynamic_index_in_dim(paired, bit, axis=1, keepdims=False))
        send = row_major(lax.dynamic_index_in_dim(paired, 1 - bit, axis=1, keepdims=False))
        pairs = [(i, i ^ step) for i in range(count)]
        got = lax.ppermute(send.astype(jnp.bfloat16), axis, pairs)
        held = row_major(keep + got.astype(jnp.float32))
        step *= 2
        if step < count <= 4 * step:
            break
    if step == count:
        return held[0], companions
    spots = count // step
    own = index // step
    total = lax.dynamic_index_in_dim(held, own, keepdims=False)
    for shift in range(1, spots):
        send = lax.dynamic_index_in_dim(held, own ^ shift, keepdims=False)
        pairs = [(i, i ^ (shift * step)) for i in range(count)]
        total = total + lax.ppermute(send.astype(jnp.bfloat16), axis, pairs).astype(jnp.float32)
    return total, companions


def replicated_sum(value, axis, companions):
    count = lax.axis_size(axis)
    if count & (count - 1):
        value, companions = lax.optimization_barrier((value, companions))
        return lax.psum(value.astype(jnp.bfloat16), axis).astype(jnp.float32), companions
    step = 1
    while step < count:
        mine = value.astype(jnp.bfloat16)
        pairs = [(i, i ^ step) for i in range(count)]
        value = mine.astype(jnp.float32) + lax.ppermute(mine, axis, pairs).astype(jnp.float32)
        if step == 1:
            value, companions = lax.optimization_barrier((value, companions))
        step *= 2
    return value, companions


def group_sum(values, groups):
    height_dev, width_dev, channels = values.shape
    return values.reshape(height_dev, width_dev, groups, channels // groups).sum(axis=(0, 1, 3))


def spread_groups(statistic, channels):
    return jnp.repeat(statistic, channels // statistic.shape[0])


def pad_columns(padded_rows):
    return jnp.pad(padded_rows, ((0, 0), (1, 1), (0, 0)))


def local(
    features, cotangent, norm_gain, norm_bias, weight, moment_one, moment_two, heights, widths
):
    latent = features[0]
    height_dev, width_dev, channels = latent.shape
    row_ids = lax.axis_index("space") * height_dev + jnp.arange(height_dev, dtype=jnp.int32)
    inside = (
        (row_ids < heights[0])[:, None]
        & (jnp.arange(width_dev, dtype=jnp.int32) < widths[0])[None, :]
    ).astype(jnp.float32)[..., None]
    cell_count = (heights[0] * widths[0] * (channels // GROUPS)).astype(jnp.float32)
    gathered = row_major(lax.all_gather(row_major(weight), "dp", axis=0, tiled=True))
    values = latent.astype(jnp.float32) * inside
    group_total, squares = space_sum(
        (group_sum(values, GROUPS), group_sum(values * values, GROUPS)), "space"
    )
    center = group_total / cell_count
    spread = squares / cell_count - center * center
    inverse = lax.rsqrt(spread + 1e-05)
    normed = (values - spread_groups(center, channels)) * spread_groups(inverse, channels) * inside
    before = normed * norm_gain + norm_bias
    activated = (jax.nn.silu(before) * inside).astype(jnp.bfloat16)
    act_pad = pad_columns(with_halo(activated, (("space", 0),), 1))
    act_cols = jnp.concatenate(
        [
            act_pad[row_off : row_off + height_dev, col_off : col_off + width_dev]
            for row_off in range(3)
            for col_off in range(3)
        ],
        axis=-1,
    ).reshape(height_dev * width_dev, 9 * channels)
    masked = cotangent[0] * inside.astype(jnp.bfloat16)
    cot_pad = pad_columns(with_halo(masked, (("space", 0),), 1))
    flat_cot = masked.reshape(-1, channels)
    weight_terms = lax.dot_general(
        act_cols, flat_cot, (((0,), (0,)), ((), ())), preferred_element_type=jnp.float32
    )
    weight_terms = row_major(weight_terms)
    weight_terms, cot_pad = lax.optimization_barrier((weight_terms, cot_pad))
    grad_piece, companions = halving_scatter(weight_terms, "dp", (gathered, cot_pad))
    grad_piece, (gathered, cot_pad) = replicated_sum(grad_piece, "space", companions)
    output = jnp.dot(act_cols, gathered, preferred_element_type=jnp.float32)
    block_out = (output.reshape(height_dev, width_dev, channels) * inside).astype(jnp.bfloat16)
    tap_weights = gathered.reshape(9, channels, channels)
    cot_cols = jnp.concatenate(
        [
            cot_pad[2 - row_off : 2 - row_off + height_dev, 2 - col_off : 2 - col_off + width_dev]
            for row_off in range(3)
            for col_off in range(3)
        ],
        axis=-1,
    ).reshape(height_dev * width_dev, 9 * channels)
    flipped = tap_weights.transpose(0, 2, 1).reshape(9 * channels, channels)
    upstream = jnp.dot(cot_cols, flipped, preferred_element_type=jnp.float32)
    gate_sig = jax.nn.sigmoid(before)
    silu_slope = gate_sig * (1.0 + before * (1.0 - gate_sig))
    scaled = upstream.reshape(height_dev, width_dev, channels) * silu_slope * inside * norm_gain
    local_first = group_sum(scaled, GROUPS)
    local_second = group_sum(scaled * normed, GROUPS)
    sum_first, sum_second = space_sum((local_first, local_second), "space")
    grad_piece = with_layout_constraint(grad_piece, Layout(major_to_minor=(1, 0)))
    first = sum_first / cell_count
    second = sum_second / cell_count
    input_grad = (
        spread_groups(inverse, channels)
        * (scaled - spread_groups(first, channels) - normed * spread_groups(second, channels))
        * inside
    ).astype(jnp.bfloat16)
    first_new = 0.9 * moment_one + 0.1 * grad_piece
    second_new = 0.999 * moment_two + 0.001 * grad_piece * grad_piece
    adam_update = first_new / (1.0 - 0.9**10) / (jnp.sqrt(second_new / (1.0 - 0.999**10)) + 1e-08)
    return (block_out[None], input_grad[None], grad_piece, adam_update)


def solution(mesh):
    placed = (
        P("dp", "space", None, None),
        P("dp", "space", None, None),
        P(),
        P(),
        P("dp", None),
        P("dp", None),
        P("dp", None),
        P("dp"),
        P("dp"),
    )
    return jax.shard_map(
        local,
        mesh=mesh,
        in_specs=placed,
        out_specs=(
            P("dp", "space", None, None),
            P("dp", "space", None, None),
            P("dp", None),
            P("dp", None),
        ),
        check_vma=False,
    )
```

```python
import jax
import jax.numpy as jnp
from jax import lax
from jax.experimental.layout import Layout, with_layout_constraint
from jax.sharding import PartitionSpec as P

GROUPS = 32


def with_halo(cells, sides, width):
    for axis, dim in sides:
        count = lax.axis_size(axis)
        ends = count - 1
        head = lax.slice_in_dim(cells, 0, width, axis=dim)
        tail = lax.slice_in_dim(cells, cells.shape[dim] - width, cells.shape[dim], axis=dim)
        cells = jnp.concatenate(
            [
                lax.ppermute(tail, axis, [(i, (i + 1) % count) for i in range(ends)]),
                cells,
                lax.ppermute(head, axis, [((i + 1) % count, i) for i in range(ends)]),
            ],
            axis=dim,
        )
    return cells


def space_sum(parts, axis):
    count = lax.axis_size(axis)
    if count > 4:
        return lax.psum(parts, axis)
    joined = jnp.stack(parts)
    shifted = [
        lax.ppermute(joined, axis, [(i, (i + shift) % count) for i in range(count)])
        for shift in range(1, count)
    ]
    for got in shifted:
        joined = joined + got
    return tuple(joined)


def row_major(value):
    return with_layout_constraint(value, Layout(major_to_minor=tuple(range(value.ndim))))


def halving_scatter(partial, axis, companions):
    count = lax.axis_size(axis)
    rows, channels = partial.shape[0] // count, partial.shape[1]
    if count & (count - 1):
        summed = lax.psum_scatter(
            partial.astype(jnp.bfloat16).reshape(count, rows, channels),
            axis,
            scatter_dimension=0,
            tiled=False,
        )
        return summed.astype(jnp.float32), companions
    index = lax.axis_index(axis)
    held = partial.reshape(count, rows, channels)
    step = 1
    while step < count:
        bit = (index // step) % 2
        paired = held.reshape(-1, 2, rows, channels)
        keep = row_major(lax.dynamic_index_in_dim(paired, bit, axis=1, keepdims=False))
        send = row_major(lax.dynamic_index_in_dim(paired, 1 - bit, axis=1, keepdims=False))
        pairs = [(i, i ^ step) for i in range(count)]
        got = lax.ppermute(send.astype(jnp.bfloat16), axis, pairs)
        held = row_major(keep + got.astype(jnp.float32))
        step *= 2
        if step < count <= 4 * step:
            break
    if step == count:
        return held[0], companions
    spots = count // step
    own = index // step
    total = lax.dynamic_index_in_dim(held, own, keepdims=False)
    for shift in range(1, spots):
        send = lax.dynamic_index_in_dim(held, own ^ shift, keepdims=False)
        pairs = [(i, i ^ (shift * step)) for i in range(count)]
        total = total + lax.ppermute(send.astype(jnp.bfloat16), axis, pairs).astype(jnp.float32)
    return total, companions


def replicated_sum(value, axis, companions):
    count = lax.axis_size(axis)
    if count & (count - 1):
        value, companions = lax.optimization_barrier((value, companions))
        return lax.psum(value.astype(jnp.bfloat16), axis).astype(jnp.float32), companions
    step = 1
    while step < count:
        mine = value.astype(jnp.bfloat16)
        pairs = [(i, i ^ step) for i in range(count)]
        value = mine.astype(jnp.float32) + lax.ppermute(mine, axis, pairs).astype(jnp.float32)
        if step == 1:
            value, companions = lax.optimization_barrier((value, companions))
        step *= 2
    return value, companions


def group_sum(values, groups):
    height_dev, width_dev, channels = values.shape
    return values.reshape(height_dev, width_dev, groups, channels // groups).sum(axis=(0, 1, 3))


def spread_groups(statistic, channels):
    return jnp.repeat(statistic, channels // statistic.shape[0])


def pad_columns(padded_rows):
    return jnp.pad(padded_rows, ((0, 0), (1, 1), (0, 0)))


def local(
    features, cotangent, norm_gain, norm_bias, weight, moment_one, moment_two, heights, widths
):
    latent = features[0]
    height_dev, width_dev, channels = latent.shape
    row_ids = lax.axis_index("space") * height_dev + jnp.arange(height_dev, dtype=jnp.int32)
    inside = (
        (row_ids < heights[0])[:, None]
        & (jnp.arange(width_dev, dtype=jnp.int32) < widths[0])[None, :]
    ).astype(jnp.float32)[..., None]
    cell_count = (heights[0] * widths[0] * (channels // GROUPS)).astype(jnp.float32)
    gathered = row_major(lax.all_gather(row_major(weight), "dp", axis=0, tiled=True))
    values = latent.astype(jnp.float32) * inside
    group_total, squares = space_sum(
        (group_sum(values, GROUPS), group_sum(values * values, GROUPS)), "space"
    )
    center = group_total / cell_count
    spread = squares / cell_count - center * center
    inverse = lax.rsqrt(spread + 1e-05)
    normed = (values - spread_groups(center, channels)) * spread_groups(inverse, channels) * inside
    before = normed * norm_gain + norm_bias
    activated = (jax.nn.silu(before) * inside).astype(jnp.bfloat16)
    act_pad = pad_columns(with_halo(activated, (("space", 0),), 1))
    act_cols = jnp.concatenate(
        [
            act_pad[row_off : row_off + height_dev, col_off : col_off + width_dev]
            for row_off in range(3)
            for col_off in range(3)
        ],
        axis=-1,
    ).reshape(height_dev * width_dev, 9 * channels)
    masked = cotangent[0] * inside.astype(jnp.bfloat16)
    cot_pad = pad_columns(with_halo(masked, (("space", 0),), 1))
    flat_cot = masked.reshape(-1, channels)
    weight_terms = lax.dot_general(
        act_cols, flat_cot, (((0,), (0,)), ((), ())), preferred_element_type=jnp.float32
    )
    weight_terms = row_major(weight_terms)
    grad_piece, companions = halving_scatter(weight_terms, "dp", (gathered, cot_pad))
    grad_piece, (gathered, cot_pad) = replicated_sum(grad_piece, "space", companions)
    output = jnp.dot(act_cols, gathered, preferred_element_type=jnp.float32)
    block_out = (output.reshape(height_dev, width_dev, channels) * inside).astype(jnp.bfloat16)
    tap_weights = gathered.reshape(9, channels, channels)
    cot_cols = jnp.concatenate(
        [
            cot_pad[2 - row_off : 2 - row_off + height_dev, 2 - col_off : 2 - col_off + width_dev]
            for row_off in range(3)
            for col_off in range(3)
        ],
        axis=-1,
    ).reshape(height_dev * width_dev, 9 * channels)
    flipped = tap_weights.transpose(0, 2, 1).reshape(9 * channels, channels)
    upstream = jnp.dot(cot_cols, flipped, preferred_element_type=jnp.float32)
    gate_sig = jax.nn.sigmoid(before)
    silu_slope = gate_sig * (1.0 + before * (1.0 - gate_sig))
    scaled = upstream.reshape(height_dev, width_dev, channels) * silu_slope * inside * norm_gain
    local_first = group_sum(scaled, GROUPS)
    local_second = group_sum(scaled * normed, GROUPS)
    sum_first, sum_second = space_sum((local_first, local_second), "space")
    grad_piece = row_major(grad_piece)
    first = sum_first / cell_count
    second = sum_second / cell_count
    input_grad = (
        spread_groups(inverse, channels)
        * (scaled - spread_groups(first, channels) - normed * spread_groups(second, channels))
        * inside
    ).astype(jnp.bfloat16)
    first_new = 0.9 * moment_one + 0.1 * grad_piece
    second_new = 0.999 * moment_two + 0.001 * grad_piece * grad_piece
    adam_update = first_new / (1.0 - 0.9**10) / (jnp.sqrt(second_new / (1.0 - 0.999**10)) + 1e-08)
    return (block_out[None], input_grad[None], grad_piece, adam_update)


def solution(mesh):
    placed = (
        P("dp", "space", None, None),
        P("dp", "space", None, None),
        P(),
        P(),
        P("dp", None),
        P("dp", None),
        P("dp", None),
        P("dp"),
        P("dp"),
    )
    return jax.shard_map(
        local,
        mesh=mesh,
        in_specs=placed,
        out_specs=(
            P("dp", "space", None, None),
            P("dp", "space", None, None),
            P("dp", None),
            P("dp", None),
        ),
        check_vma=False,
    )
```

```python
import jax
import jax.numpy as jnp
from jax import lax
from jax.experimental.layout import Layout, with_layout_constraint
from jax.sharding import PartitionSpec as P

GROUPS = 32


def with_halo(cells, sides, width):
    for axis, dim in sides:
        count = lax.axis_size(axis)
        ends = count - 1
        head = lax.slice_in_dim(cells, 0, width, axis=dim)
        tail = lax.slice_in_dim(cells, cells.shape[dim] - width, cells.shape[dim], axis=dim)
        cells = jnp.concatenate(
            [
                lax.ppermute(tail, axis, [(i, (i + 1) % count) for i in range(ends)]),
                cells,
                lax.ppermute(head, axis, [((i + 1) % count, i) for i in range(ends)]),
            ],
            axis=dim,
        )
    return cells


def space_sum(parts, axis):
    count = lax.axis_size(axis)
    if count > 4:
        return lax.psum(parts, axis)
    joined = jnp.stack(parts)
    shifted = [
        lax.ppermute(joined, axis, [(i, (i + shift) % count) for i in range(count)])
        for shift in range(1, count)
    ]
    for got in shifted:
        joined = joined + got
    return tuple(joined)


def row_major(value):
    return with_layout_constraint(value, Layout(major_to_minor=tuple(range(value.ndim))))


def halving_scatter(partial, axis, companions):
    count = lax.axis_size(axis)
    rows, channels = partial.shape[0] // count, partial.shape[1]
    if count & (count - 1):
        summed = lax.psum_scatter(
            partial.astype(jnp.bfloat16).reshape(count, rows, channels),
            axis,
            scatter_dimension=0,
            tiled=False,
        )
        return summed.astype(jnp.float32), companions
    index = lax.axis_index(axis)
    held = partial.reshape(count, rows, channels)
    step = 1
    while step < count:
        bit = (index // step) % 2
        paired = held.reshape(-1, 2, rows, channels)
        keep = row_major(lax.dynamic_index_in_dim(paired, bit, axis=1, keepdims=False))
        send = row_major(lax.dynamic_index_in_dim(paired, 1 - bit, axis=1, keepdims=False))
        pairs = [(i, i ^ step) for i in range(count)]
        got = lax.ppermute(send.astype(jnp.bfloat16), axis, pairs)
        held = row_major(keep + got.astype(jnp.float32))
        step *= 2
        if step < count <= 4 * step:
            break
    if step == count:
        return held[0], companions
    spots = count // step
    own = index // step
    total = lax.dynamic_index_in_dim(held, own, keepdims=False)
    for shift in range(1, spots):
        send = lax.dynamic_index_in_dim(held, own ^ shift, keepdims=False)
        pairs = [(i, i ^ (shift * step)) for i in range(count)]
        total = total + lax.ppermute(send.astype(jnp.bfloat16), axis, pairs).astype(jnp.float32)
    return total, companions


def replicated_sum(value, axis, companions):
    count = lax.axis_size(axis)
    if count & (count - 1):
        value, companions = lax.optimization_barrier((value, companions))
        return lax.psum(value.astype(jnp.bfloat16), axis).astype(jnp.float32), companions
    step = count // 2
    while step:
        mine = value.astype(jnp.bfloat16)
        pairs = [(i, i ^ step) for i in range(count)]
        value = mine.astype(jnp.float32) + lax.ppermute(mine, axis, pairs).astype(jnp.float32)
        if step * 2 == count:
            value, companions = lax.optimization_barrier((value, companions))
        step //= 2
    return value, companions


def group_sum(values, groups):
    height_dev, width_dev, channels = values.shape
    return values.reshape(height_dev, width_dev, groups, channels // groups).sum(axis=(0, 1, 3))


def spread_groups(statistic, channels):
    return jnp.repeat(statistic, channels // statistic.shape[0])


def pad_columns(padded_rows):
    return jnp.pad(padded_rows, ((0, 0), (1, 1), (0, 0)))


def local(
    features, cotangent, norm_gain, norm_bias, weight, moment_one, moment_two, heights, widths
):
    latent = features[0]
    height_dev, width_dev, channels = latent.shape
    row_ids = lax.axis_index("space") * height_dev + jnp.arange(height_dev, dtype=jnp.int32)
    inside = (
        (row_ids < heights[0])[:, None]
        & (jnp.arange(width_dev, dtype=jnp.int32) < widths[0])[None, :]
    ).astype(jnp.float32)[..., None]
    cell_count = (heights[0] * widths[0] * (channels // GROUPS)).astype(jnp.float32)
    gathered = row_major(lax.all_gather(row_major(weight), "dp", axis=0, tiled=True))
    values = latent.astype(jnp.float32) * inside
    group_total, squares = space_sum(
        (group_sum(values, GROUPS), group_sum(values * values, GROUPS)), "space"
    )
    center = group_total / cell_count
    spread = squares / cell_count - center * center
    inverse = lax.rsqrt(spread + 1e-05)
    normed = (values - spread_groups(center, channels)) * spread_groups(inverse, channels) * inside
    before = normed * norm_gain + norm_bias
    activated = (jax.nn.silu(before) * inside).astype(jnp.bfloat16)
    act_pad = pad_columns(with_halo(activated, (("space", 0),), 1))
    act_cols = jnp.concatenate(
        [
            act_pad[row_off : row_off + height_dev, col_off : col_off + width_dev]
            for row_off in range(3)
            for col_off in range(3)
        ],
        axis=-1,
    ).reshape(height_dev * width_dev, 9 * channels)
    masked = cotangent[0] * inside.astype(jnp.bfloat16)
    cot_pad = pad_columns(with_halo(masked, (("space", 0),), 1))
    flat_cot = masked.reshape(-1, channels)
    weight_terms = lax.dot_general(
        act_cols, flat_cot, (((0,), (0,)), ((), ())), preferred_element_type=jnp.float32
    )
    weight_terms = row_major(weight_terms)
    grad_piece, companions = halving_scatter(weight_terms, "dp", (gathered, cot_pad))
    grad_piece, (gathered, cot_pad) = replicated_sum(grad_piece, "space", companions)
    output = jnp.dot(act_cols, gathered, preferred_element_type=jnp.float32)
    block_out = (output.reshape(height_dev, width_dev, channels) * inside).astype(jnp.bfloat16)
    tap_weights = gathered.reshape(9, channels, channels)
    cot_cols = jnp.concatenate(
        [
            cot_pad[2 - row_off : 2 - row_off + height_dev, 2 - col_off : 2 - col_off + width_dev]
            for row_off in range(3)
            for col_off in range(3)
        ],
        axis=-1,
    ).reshape(height_dev * width_dev, 9 * channels)
    flipped = tap_weights.transpose(0, 2, 1).reshape(9 * channels, channels)
    upstream = jnp.dot(cot_cols, flipped, preferred_element_type=jnp.float32)
    gate_sig = jax.nn.sigmoid(before)
    silu_slope = gate_sig * (1.0 + before * (1.0 - gate_sig))
    scaled = upstream.reshape(height_dev, width_dev, channels) * silu_slope * inside * norm_gain
    local_first = group_sum(scaled, GROUPS)
    local_second = group_sum(scaled * normed, GROUPS)
    sum_first, sum_second = space_sum((local_first, local_second), "space")
    grad_piece = with_layout_constraint(grad_piece, Layout(major_to_minor=(1, 0)))
    first = sum_first / cell_count
    second = sum_second / cell_count
    input_grad = (
        spread_groups(inverse, channels)
        * (scaled - spread_groups(first, channels) - normed * spread_groups(second, channels))
        * inside
    ).astype(jnp.bfloat16)
    first_new = 0.9 * moment_one + 0.1 * grad_piece
    second_new = 0.999 * moment_two + 0.001 * grad_piece * grad_piece
    adam_update = first_new / (1.0 - 0.9**10) / (jnp.sqrt(second_new / (1.0 - 0.999**10)) + 1e-08)
    return (block_out[None], input_grad[None], grad_piece, adam_update)


def solution(mesh):
    placed = (
        P("dp", "space", None, None),
        P("dp", "space", None, None),
        P(),
        P(),
        P("dp", None),
        P("dp", None),
        P("dp", None),
        P("dp"),
        P("dp"),
    )
    return jax.shard_map(
        local,
        mesh=mesh,
        in_specs=placed,
        out_specs=(
            P("dp", "space", None, None),
            P("dp", "space", None, None),
            P("dp", None),
            P("dp", None),
        ),
        check_vma=False,
    )
```

```python
import jax
import jax.numpy as jnp
from jax import lax
from jax.experimental.layout import Layout, with_layout_constraint
from jax.sharding import PartitionSpec as P

GROUPS = 32


def with_halo(cells, sides, width):
    for axis, dim in sides:
        count = lax.axis_size(axis)
        ends = count - 1
        head = lax.slice_in_dim(cells, 0, width, axis=dim)
        tail = lax.slice_in_dim(cells, cells.shape[dim] - width, cells.shape[dim], axis=dim)
        cells = jnp.concatenate(
            [
                lax.ppermute(tail, axis, [(i, (i + 1) % count) for i in range(ends)]),
                cells,
                lax.ppermute(head, axis, [((i + 1) % count, i) for i in range(ends)]),
            ],
            axis=dim,
        )
    return cells


def space_sum(parts, axis):
    count = lax.axis_size(axis)
    if count > 4:
        return lax.psum(parts, axis)
    joined = jnp.stack(parts)
    shifted = [
        lax.ppermute(joined, axis, [(i, (i + shift) % count) for i in range(count)])
        for shift in range(1, count)
    ]
    for got in shifted:
        joined = joined + got
    return tuple(joined)


def row_major(value):
    return with_layout_constraint(value, Layout(major_to_minor=tuple(range(value.ndim))))


def halving_scatter(partial, axis, companions):
    count = lax.axis_size(axis)
    rows, channels = partial.shape[0] // count, partial.shape[1]
    if count & (count - 1):
        summed = lax.psum_scatter(
            partial.astype(jnp.bfloat16).reshape(count, rows, channels),
            axis,
            scatter_dimension=0,
            tiled=False,
        )
        return summed.astype(jnp.float32), companions
    index = lax.axis_index(axis)
    held = partial.reshape(count, rows, channels)
    step = 1
    while step < count:
        bit = (index // step) % 2
        paired = held.reshape(-1, 2, rows, channels)
        keep = row_major(lax.dynamic_index_in_dim(paired, bit, axis=1, keepdims=False))
        send = row_major(lax.dynamic_index_in_dim(paired, 1 - bit, axis=1, keepdims=False))
        pairs = [(i, i ^ step) for i in range(count)]
        got = lax.ppermute(send.astype(jnp.bfloat16), axis, pairs)
        held = row_major(keep + got.astype(jnp.float32))
        if step == 1:
            held, companions = lax.optimization_barrier((held, companions))
        step *= 2
        if step < count <= 4 * step:
            break
    if step == count:
        return held[0], companions
    spots = count // step
    own = index // step
    total = lax.dynamic_index_in_dim(held, own, keepdims=False)
    for shift in range(1, spots):
        send = lax.dynamic_index_in_dim(held, own ^ shift, keepdims=False)
        pairs = [(i, i ^ (shift * step)) for i in range(count)]
        total = total + lax.ppermute(send.astype(jnp.bfloat16), axis, pairs).astype(jnp.float32)
    return total, companions


def replicated_sum(value, axis, companions):
    count = lax.axis_size(axis)
    if count & (count - 1):
        value, companions = lax.optimization_barrier((value, companions))
        return lax.psum(value.astype(jnp.bfloat16), axis).astype(jnp.float32), companions
    step = count // 2
    while step:
        mine = value.astype(jnp.bfloat16)
        pairs = [(i, i ^ step) for i in range(count)]
        value = mine.astype(jnp.float32) + lax.ppermute(mine, axis, pairs).astype(jnp.float32)
        if step * 2 == count:
            value, companions = lax.optimization_barrier((value, companions))
        step //= 2
    return value, companions


def group_sum(values, groups):
    height_dev, width_dev, channels = values.shape
    return values.reshape(height_dev, width_dev, groups, channels // groups).sum(axis=(0, 1, 3))


def spread_groups(statistic, channels):
    return jnp.repeat(statistic, channels // statistic.shape[0])


def pad_columns(padded_rows):
    return jnp.pad(padded_rows, ((0, 0), (1, 1), (0, 0)))


def local(
    features, cotangent, norm_gain, norm_bias, weight, moment_one, moment_two, heights, widths
):
    latent = features[0]
    height_dev, width_dev, channels = latent.shape
    row_ids = lax.axis_index("space") * height_dev + jnp.arange(height_dev, dtype=jnp.int32)
    inside = (
        (row_ids < heights[0])[:, None]
        & (jnp.arange(width_dev, dtype=jnp.int32) < widths[0])[None, :]
    ).astype(jnp.float32)[..., None]
    cell_count = (heights[0] * widths[0] * (channels // GROUPS)).astype(jnp.float32)
    gathered = row_major(lax.all_gather(row_major(weight), "dp", axis=0, tiled=True))
    values = latent.astype(jnp.float32) * inside
    group_total, squares = space_sum(
        (group_sum(values, GROUPS), group_sum(values * values, GROUPS)), "space"
    )
    center = group_total / cell_count
    spread = squares / cell_count - center * center
    inverse = lax.rsqrt(spread + 1e-05)
    normed = (values - spread_groups(center, channels)) * spread_groups(inverse, channels) * inside
    before = normed * norm_gain + norm_bias
    activated = (jax.nn.silu(before) * inside).astype(jnp.bfloat16)
    act_pad = pad_columns(with_halo(activated, (("space", 0),), 1))
    act_cols = jnp.concatenate(
        [
            act_pad[row_off : row_off + height_dev, col_off : col_off + width_dev]
            for row_off in range(3)
            for col_off in range(3)
        ],
        axis=-1,
    ).reshape(height_dev * width_dev, 9 * channels)
    masked = cotangent[0] * inside.astype(jnp.bfloat16)
    cot_pad = pad_columns(with_halo(masked, (("space", 0),), 1))
    flat_cot = masked.reshape(-1, channels)
    weight_terms = lax.dot_general(
        act_cols, flat_cot, (((0,), (0,)), ((), ())), preferred_element_type=jnp.float32
    )
    weight_terms = row_major(weight_terms)
    grad_piece, cot_pad = halving_scatter(weight_terms, "dp", cot_pad)
    grad_piece, (gathered, cot_pad) = replicated_sum(grad_piece, "space", (gathered, cot_pad))
    output = jnp.dot(act_cols, gathered, preferred_element_type=jnp.float32)
    block_out = (output.reshape(height_dev, width_dev, channels) * inside).astype(jnp.bfloat16)
    tap_weights = gathered.reshape(9, channels, channels)
    cot_cols = jnp.concatenate(
        [
            cot_pad[2 - row_off : 2 - row_off + height_dev, 2 - col_off : 2 - col_off + width_dev]
            for row_off in range(3)
            for col_off in range(3)
        ],
        axis=-1,
    ).reshape(height_dev * width_dev, 9 * channels)
    flipped = tap_weights.transpose(0, 2, 1).reshape(9 * channels, channels)
    upstream = jnp.dot(cot_cols, flipped, preferred_element_type=jnp.float32)
    gate_sig = jax.nn.sigmoid(before)
    silu_slope = gate_sig * (1.0 + before * (1.0 - gate_sig))
    scaled = upstream.reshape(height_dev, width_dev, channels) * silu_slope * inside * norm_gain
    local_first = group_sum(scaled, GROUPS)
    local_second = group_sum(scaled * normed, GROUPS)
    sum_first, sum_second = space_sum((local_first, local_second), "space")
    grad_piece = with_layout_constraint(grad_piece, Layout(major_to_minor=(1, 0)))
    first = sum_first / cell_count
    second = sum_second / cell_count
    input_grad = (
        spread_groups(inverse, channels)
        * (scaled - spread_groups(first, channels) - normed * spread_groups(second, channels))
        * inside
    ).astype(jnp.bfloat16)
    first_new = 0.9 * moment_one + 0.1 * grad_piece
    second_new = 0.999 * moment_two + 0.001 * grad_piece * grad_piece
    adam_update = first_new / (1.0 - 0.9**10) / (jnp.sqrt(second_new / (1.0 - 0.999**10)) + 1e-08)
    return (block_out[None], input_grad[None], grad_piece, adam_update)


def solution(mesh):
    placed = (
        P("dp", "space", None, None),
        P("dp", "space", None, None),
        P(),
        P(),
        P("dp", None),
        P("dp", None),
        P("dp", None),
        P("dp"),
        P("dp"),
    )
    return jax.shard_map(
        local,
        mesh=mesh,
        in_specs=placed,
        out_specs=(
            P("dp", "space", None, None),
            P("dp", "space", None, None),
            P("dp", None),
            P("dp", None),
        ),
        check_vma=False,
    )
```

```python
import jax
import jax.numpy as jnp
from jax import lax
from jax.experimental.layout import Layout, with_layout_constraint
from jax.sharding import PartitionSpec as P

GROUPS = 32


def with_halo(cells, sides, width):
    for axis, dim in sides:
        count = lax.axis_size(axis)
        ends = count - 1
        head = lax.slice_in_dim(cells, 0, width, axis=dim)
        tail = lax.slice_in_dim(cells, cells.shape[dim] - width, cells.shape[dim], axis=dim)
        cells = jnp.concatenate(
            [
                lax.ppermute(tail, axis, [(i, (i + 1) % count) for i in range(ends)]),
                cells,
                lax.ppermute(head, axis, [((i + 1) % count, i) for i in range(ends)]),
            ],
            axis=dim,
        )
    return cells


def space_sum(parts, axis):
    count = lax.axis_size(axis)
    if count > 4:
        return lax.psum(parts, axis)
    joined = jnp.stack(parts)
    shifted = [
        lax.ppermute(joined, axis, [(i, (i + shift) % count) for i in range(count)])
        for shift in range(1, count)
    ]
    for got in shifted:
        joined = joined + got
    return tuple(joined)


def row_major(value):
    return with_layout_constraint(value, Layout(major_to_minor=tuple(range(value.ndim))))


def halving_scatter(partial, axis, companions):
    count = lax.axis_size(axis)
    rows, channels = partial.shape[0] // count, partial.shape[1]
    if count & (count - 1):
        summed = lax.psum_scatter(
            partial.astype(jnp.bfloat16).reshape(count, rows, channels),
            axis,
            scatter_dimension=0,
            tiled=False,
        )
        return summed.astype(jnp.float32), companions
    index = lax.axis_index(axis)
    held = partial.reshape(count, rows, channels)
    step = 1
    while step < count:
        bit = (index // step) % 2
        paired = held.reshape(-1, 2, rows, channels)
        keep = row_major(lax.dynamic_index_in_dim(paired, bit, axis=1, keepdims=False))
        send = row_major(lax.dynamic_index_in_dim(paired, 1 - bit, axis=1, keepdims=False))
        pairs = [(i, i ^ step) for i in range(count)]
        got = lax.ppermute(send.astype(jnp.bfloat16), axis, pairs)
        held = row_major(keep.astype(jnp.float32) + got.astype(jnp.float32))
        step *= 2
        if step < count <= 4 * step:
            break
    if step == count:
        return held[0], companions
    spots = count // step
    own = index // step
    total = lax.dynamic_index_in_dim(held, own, keepdims=False)
    for shift in range(1, spots):
        send = lax.dynamic_index_in_dim(held, own ^ shift, keepdims=False)
        pairs = [(i, i ^ (shift * step)) for i in range(count)]
        total = total + lax.ppermute(send.astype(jnp.bfloat16), axis, pairs).astype(jnp.float32)
    return total, companions


def replicated_sum(value, axis, companions):
    count = lax.axis_size(axis)
    if count & (count - 1):
        value, companions = lax.optimization_barrier((value, companions))
        return lax.psum(value.astype(jnp.bfloat16), axis).astype(jnp.float32), companions
    step = 1
    while step < count:
        mine = value.astype(jnp.bfloat16)
        pairs = [(i, i ^ step) for i in range(count)]
        value = mine.astype(jnp.float32) + lax.ppermute(mine, axis, pairs).astype(jnp.float32)
        if step == 1:
            value, companions = lax.optimization_barrier((value, companions))
        step *= 2
    return value, companions


def group_sum(values, groups):
    height_dev, width_dev, channels = values.shape
    return values.reshape(height_dev, width_dev, groups, channels // groups).sum(axis=(0, 1, 3))


def spread_groups(statistic, channels):
    return jnp.repeat(statistic, channels // statistic.shape[0])


def pad_columns(padded_rows):
    return jnp.pad(padded_rows, ((0, 0), (1, 1), (0, 0)))


def local(
    features, cotangent, norm_gain, norm_bias, weight, moment_one, moment_two, heights, widths
):
    latent = features[0]
    height_dev, width_dev, channels = latent.shape
    row_ids = lax.axis_index("space") * height_dev + jnp.arange(height_dev, dtype=jnp.int32)
    inside = (
        (row_ids < heights[0])[:, None]
        & (jnp.arange(width_dev, dtype=jnp.int32) < widths[0])[None, :]
    ).astype(jnp.float32)[..., None]
    cell_count = (heights[0] * widths[0] * (channels // GROUPS)).astype(jnp.float32)
    gathered = row_major(lax.all_gather(row_major(weight), "dp", axis=0, tiled=True))
    values = latent.astype(jnp.float32) * inside
    group_total, squares = space_sum(
        (group_sum(values, GROUPS), group_sum(values * values, GROUPS)), "space"
    )
    center = group_total / cell_count
    spread = squares / cell_count - center * center
    inverse = lax.rsqrt(spread + 1e-05)
    normed = (values - spread_groups(center, channels)) * spread_groups(inverse, channels) * inside
    before = normed * norm_gain + norm_bias
    activated = (jax.nn.silu(before) * inside).astype(jnp.bfloat16)
    act_pad = pad_columns(with_halo(activated, (("space", 0),), 1))
    act_cols = jnp.concatenate(
        [
            act_pad[row_off : row_off + height_dev, col_off : col_off + width_dev]
            for row_off in range(3)
            for col_off in range(3)
        ],
        axis=-1,
    ).reshape(height_dev * width_dev, 9 * channels)
    masked = cotangent[0] * inside.astype(jnp.bfloat16)
    cot_pad = pad_columns(with_halo(masked, (("space", 0),), 1))
    flat_cot = masked.reshape(-1, channels)
    weight_terms = lax.dot_general(
        act_cols, flat_cot, (((0,), (0,)), ((), ())), preferred_element_type=jnp.float32
    ).astype(jnp.bfloat16)
    weight_terms = row_major(weight_terms)
    grad_piece, companions = halving_scatter(weight_terms, "dp", (gathered, cot_pad))
    grad_piece, (gathered, cot_pad) = replicated_sum(grad_piece, "space", companions)
    output = jnp.dot(act_cols, gathered, preferred_element_type=jnp.float32)
    block_out = (output.reshape(height_dev, width_dev, channels) * inside).astype(jnp.bfloat16)
    tap_weights = gathered.reshape(9, channels, channels)
    cot_cols = jnp.concatenate(
        [
            cot_pad[2 - row_off : 2 - row_off + height_dev, 2 - col_off : 2 - col_off + width_dev]
            for row_off in range(3)
            for col_off in range(3)
        ],
        axis=-1,
    ).reshape(height_dev * width_dev, 9 * channels)
    flipped = tap_weights.transpose(0, 2, 1).reshape(9 * channels, channels)
    upstream = jnp.dot(cot_cols, flipped, preferred_element_type=jnp.float32)
    gate_sig = jax.nn.sigmoid(before)
    silu_slope = gate_sig * (1.0 + before * (1.0 - gate_sig))
    scaled = upstream.reshape(height_dev, width_dev, channels) * silu_slope * inside * norm_gain
    local_first = group_sum(scaled, GROUPS)
    local_second = group_sum(scaled * normed, GROUPS)
    sum_first, sum_second = space_sum((local_first, local_second), "space")
    grad_piece = with_layout_constraint(grad_piece, Layout(major_to_minor=(1, 0)))
    first = sum_first / cell_count
    second = sum_second / cell_count
    input_grad = (
        spread_groups(inverse, channels)
        * (scaled - spread_groups(first, channels) - normed * spread_groups(second, channels))
        * inside
    ).astype(jnp.bfloat16)
    first_new = 0.9 * moment_one + 0.1 * grad_piece
    second_new = 0.999 * moment_two + 0.001 * grad_piece * grad_piece
    adam_update = first_new / (1.0 - 0.9**10) / (jnp.sqrt(second_new / (1.0 - 0.999**10)) + 1e-08)
    return (block_out[None], input_grad[None], grad_piece, adam_update)


def solution(mesh):
    placed = (
        P("dp", "space", None, None),
        P("dp", "space", None, None),
        P(),
        P(),
        P("dp", None),
        P("dp", None),
        P("dp", None),
        P("dp"),
        P("dp"),
    )
    return jax.shard_map(
        local,
        mesh=mesh,
        in_specs=placed,
        out_specs=(
            P("dp", "space", None, None),
            P("dp", "space", None, None),
            P("dp", None),
            P("dp", None),
        ),
        check_vma=False,
    )
```

```python
import jax
import jax.numpy as jnp
from jax import lax
from jax.experimental.layout import Layout, with_layout_constraint
from jax.sharding import PartitionSpec as P

GROUPS = 32


def with_halo(cells, sides, width):
    for axis, dim in sides:
        count = lax.axis_size(axis)
        ends = count - 1
        head = lax.slice_in_dim(cells, 0, width, axis=dim)
        tail = lax.slice_in_dim(cells, cells.shape[dim] - width, cells.shape[dim], axis=dim)
        cells = jnp.concatenate(
            [
                lax.ppermute(tail, axis, [(i, (i + 1) % count) for i in range(ends)]),
                cells,
                lax.ppermute(head, axis, [((i + 1) % count, i) for i in range(ends)]),
            ],
            axis=dim,
        )
    return cells


def space_sum(parts, axis):
    count = lax.axis_size(axis)
    if count > 4:
        return lax.psum(parts, axis)
    joined = jnp.stack(parts)
    shifted = [
        lax.ppermute(joined, axis, [(i, (i + shift) % count) for i in range(count)])
        for shift in range(1, count)
    ]
    for got in shifted:
        joined = joined + got
    return tuple(joined)


def row_major(value):
    return with_layout_constraint(value, Layout(major_to_minor=tuple(range(value.ndim))))


def halving_scatter(partial, axis, companions):
    count = lax.axis_size(axis)
    rows, channels = partial.shape[0] // count, partial.shape[1]
    if count & (count - 1):
        summed = lax.psum_scatter(
            partial.astype(jnp.bfloat16).reshape(count, rows, channels),
            axis,
            scatter_dimension=0,
            tiled=False,
        )
        return summed.astype(jnp.float32), companions
    index = lax.axis_index(axis)
    held = partial.reshape(count, rows, channels)
    step = 1
    while step < count:
        bit = (index // step) % 2
        paired = held.reshape(-1, 2, rows, channels)
        keep = row_major(lax.dynamic_index_in_dim(paired, bit, axis=1, keepdims=False))
        send = row_major(lax.dynamic_index_in_dim(paired, 1 - bit, axis=1, keepdims=False))
        pairs = [(i, i ^ step) for i in range(count)]
        got = lax.ppermute(send.astype(jnp.bfloat16), axis, pairs)
        held = row_major((keep.astype(jnp.float32) + got.astype(jnp.float32)).astype(jnp.bfloat16))
        step *= 2
        if step < count <= 4 * step:
            break
    if step == count:
        return held[0].astype(jnp.float32), companions
    spots = count // step
    own = index // step
    total = lax.dynamic_index_in_dim(held, own, keepdims=False).astype(jnp.float32)
    for shift in range(1, spots):
        send = lax.dynamic_index_in_dim(held, own ^ shift, keepdims=False)
        pairs = [(i, i ^ (shift * step)) for i in range(count)]
        total = total + lax.ppermute(send.astype(jnp.bfloat16), axis, pairs).astype(jnp.float32)
    return total, companions


def replicated_sum(value, axis, companions):
    count = lax.axis_size(axis)
    if count & (count - 1):
        value, companions = lax.optimization_barrier((value, companions))
        return lax.psum(value.astype(jnp.bfloat16), axis).astype(jnp.float32), companions
    step = 1
    while step < count:
        mine = value.astype(jnp.bfloat16)
        pairs = [(i, i ^ step) for i in range(count)]
        value = mine.astype(jnp.float32) + lax.ppermute(mine, axis, pairs).astype(jnp.float32)
        if step == 1:
            value, companions = lax.optimization_barrier((value, companions))
        step *= 2
    return value, companions


def group_sum(values, groups):
    height_dev, width_dev, channels = values.shape
    return values.reshape(height_dev, width_dev, groups, channels // groups).sum(axis=(0, 1, 3))


def spread_groups(statistic, channels):
    return jnp.repeat(statistic, channels // statistic.shape[0])


def pad_columns(padded_rows):
    return jnp.pad(padded_rows, ((0, 0), (1, 1), (0, 0)))


def local(
    features, cotangent, norm_gain, norm_bias, weight, moment_one, moment_two, heights, widths
):
    latent = features[0]
    height_dev, width_dev, channels = latent.shape
    row_ids = lax.axis_index("space") * height_dev + jnp.arange(height_dev, dtype=jnp.int32)
    inside = (
        (row_ids < heights[0])[:, None]
        & (jnp.arange(width_dev, dtype=jnp.int32) < widths[0])[None, :]
    ).astype(jnp.float32)[..., None]
    cell_count = (heights[0] * widths[0] * (channels // GROUPS)).astype(jnp.float32)
    gathered = row_major(lax.all_gather(row_major(weight), "dp", axis=0, tiled=True))
    values = latent.astype(jnp.float32) * inside
    group_total, squares = space_sum(
        (group_sum(values, GROUPS), group_sum(values * values, GROUPS)), "space"
    )
    center = group_total / cell_count
    spread = squares / cell_count - center * center
    inverse = lax.rsqrt(spread + 1e-05)
    normed = (values - spread_groups(center, channels)) * spread_groups(inverse, channels) * inside
    before = normed * norm_gain + norm_bias
    activated = (jax.nn.silu(before) * inside).astype(jnp.bfloat16)
    act_pad = pad_columns(with_halo(activated, (("space", 0),), 1))
    act_cols = jnp.concatenate(
        [
            act_pad[row_off : row_off + height_dev, col_off : col_off + width_dev]
            for row_off in range(3)
            for col_off in range(3)
        ],
        axis=-1,
    ).reshape(height_dev * width_dev, 9 * channels)
    masked = cotangent[0] * inside.astype(jnp.bfloat16)
    cot_pad = pad_columns(with_halo(masked, (("space", 0),), 1))
    flat_cot = masked.reshape(-1, channels)
    weight_terms = lax.dot_general(
        act_cols, flat_cot, (((0,), (0,)), ((), ())), preferred_element_type=jnp.float32
    ).astype(jnp.bfloat16)
    weight_terms = row_major(weight_terms)
    grad_piece, companions = halving_scatter(weight_terms, "dp", (gathered, cot_pad))
    grad_piece, (gathered, cot_pad) = replicated_sum(grad_piece, "space", companions)
    output = jnp.dot(act_cols, gathered, preferred_element_type=jnp.float32)
    block_out = (output.reshape(height_dev, width_dev, channels) * inside).astype(jnp.bfloat16)
    tap_weights = gathered.reshape(9, channels, channels)
    cot_cols = jnp.concatenate(
        [
            cot_pad[2 - row_off : 2 - row_off + height_dev, 2 - col_off : 2 - col_off + width_dev]
            for row_off in range(3)
            for col_off in range(3)
        ],
        axis=-1,
    ).reshape(height_dev * width_dev, 9 * channels)
    flipped = tap_weights.transpose(0, 2, 1).reshape(9 * channels, channels)
    upstream = jnp.dot(cot_cols, flipped, preferred_element_type=jnp.float32)
    gate_sig = jax.nn.sigmoid(before)
    silu_slope = gate_sig * (1.0 + before * (1.0 - gate_sig))
    scaled = upstream.reshape(height_dev, width_dev, channels) * silu_slope * inside * norm_gain
    local_first = group_sum(scaled, GROUPS)
    local_second = group_sum(scaled * normed, GROUPS)
    sum_first, sum_second = space_sum((local_first, local_second), "space")
    grad_piece = with_layout_constraint(grad_piece, Layout(major_to_minor=(1, 0)))
    first = sum_first / cell_count
    second = sum_second / cell_count
    input_grad = (
        spread_groups(inverse, channels)
        * (scaled - spread_groups(first, channels) - normed * spread_groups(second, channels))
        * inside
    ).astype(jnp.bfloat16)
    first_new = 0.9 * moment_one + 0.1 * grad_piece
    second_new = 0.999 * moment_two + 0.001 * grad_piece * grad_piece
    adam_update = first_new / (1.0 - 0.9**10) / (jnp.sqrt(second_new / (1.0 - 0.999**10)) + 1e-08)
    return (block_out[None], input_grad[None], grad_piece, adam_update)


def solution(mesh):
    placed = (
        P("dp", "space", None, None),
        P("dp", "space", None, None),
        P(),
        P(),
        P("dp", None),
        P("dp", None),
        P("dp", None),
        P("dp"),
        P("dp"),
    )
    return jax.shard_map(
        local,
        mesh=mesh,
        in_specs=placed,
        out_specs=(
            P("dp", "space", None, None),
            P("dp", "space", None, None),
            P("dp", None),
            P("dp", None),
        ),
        check_vma=False,
    )
```

```python
import jax
import jax.numpy as jnp
from jax import lax
from jax.experimental.layout import Layout, with_layout_constraint
from jax.sharding import PartitionSpec as P

GROUPS = 32


def with_halo(cells, sides, width):
    for axis, dim in sides:
        count = lax.axis_size(axis)
        ends = count - 1
        head = lax.slice_in_dim(cells, 0, width, axis=dim)
        tail = lax.slice_in_dim(cells, cells.shape[dim] - width, cells.shape[dim], axis=dim)
        cells = jnp.concatenate(
            [
                lax.ppermute(tail, axis, [(i, (i + 1) % count) for i in range(ends)]),
                cells,
                lax.ppermute(head, axis, [((i + 1) % count, i) for i in range(ends)]),
            ],
            axis=dim,
        )
    return cells


def space_sum(parts, axis):
    count = lax.axis_size(axis)
    if count > 4:
        return lax.psum(parts, axis)
    joined = jnp.stack(parts)
    shifted = [
        lax.ppermute(joined, axis, [(i, (i + shift) % count) for i in range(count)])
        for shift in range(1, count)
    ]
    for got in shifted:
        joined = joined + got
    return tuple(joined)


def row_major(value):
    return with_layout_constraint(value, Layout(major_to_minor=tuple(range(value.ndim))))


def halving_scatter(partial, axis, companions):
    count = lax.axis_size(axis)
    rows, channels = partial.shape[0] // count, partial.shape[1]
    if count & (count - 1):
        summed = lax.psum_scatter(
            partial.astype(jnp.bfloat16).reshape(count, rows, channels),
            axis,
            scatter_dimension=0,
            tiled=False,
        )
        return summed.astype(jnp.float32), companions
    index = lax.axis_index(axis)
    held = partial.reshape(count, rows, channels)
    step = 1
    while step < count:
        bit = (index // step) % 2
        paired = held.reshape(-1, 2, rows, channels)
        keep = lax.dynamic_index_in_dim(paired, bit, axis=1, keepdims=False)
        send = lax.dynamic_index_in_dim(paired, 1 - bit, axis=1, keepdims=False)
        pairs = [(i, i ^ step) for i in range(count)]
        got = lax.ppermute(send.astype(jnp.bfloat16), axis, pairs)
        held = (keep.astype(jnp.float32) + got.astype(jnp.float32)).astype(jnp.bfloat16)
        step *= 2
        if step < count <= 4 * step:
            break
    if step == count:
        return held[0].astype(jnp.float32), companions
    spots = count // step
    own = index // step
    total = lax.dynamic_index_in_dim(held, own, keepdims=False).astype(jnp.float32)
    for shift in range(1, spots):
        send = lax.dynamic_index_in_dim(held, own ^ shift, keepdims=False)
        pairs = [(i, i ^ (shift * step)) for i in range(count)]
        total = total + lax.ppermute(send.astype(jnp.bfloat16), axis, pairs).astype(jnp.float32)
    return total, companions


def replicated_sum(value, axis, companions):
    count = lax.axis_size(axis)
    if count & (count - 1):
        value, companions = lax.optimization_barrier((value, companions))
        return lax.psum(value.astype(jnp.bfloat16), axis).astype(jnp.float32), companions
    step = 1
    while step < count:
        mine = value.astype(jnp.bfloat16)
        pairs = [(i, i ^ step) for i in range(count)]
        value = mine.astype(jnp.float32) + lax.ppermute(mine, axis, pairs).astype(jnp.float32)
        if step == 1:
            value, companions = lax.optimization_barrier((value, companions))
        step *= 2
    return value, companions


def group_sum(values, groups):
    height_dev, width_dev, channels = values.shape
    return values.reshape(height_dev, width_dev, groups, channels // groups).sum(axis=(0, 1, 3))


def spread_groups(statistic, channels):
    return jnp.repeat(statistic, channels // statistic.shape[0])


def pad_columns(padded_rows):
    return jnp.pad(padded_rows, ((0, 0), (1, 1), (0, 0)))


def local(
    features, cotangent, norm_gain, norm_bias, weight, moment_one, moment_two, heights, widths
):
    latent = features[0]
    height_dev, width_dev, channels = latent.shape
    row_ids = lax.axis_index("space") * height_dev + jnp.arange(height_dev, dtype=jnp.int32)
    inside = (
        (row_ids < heights[0])[:, None]
        & (jnp.arange(width_dev, dtype=jnp.int32) < widths[0])[None, :]
    ).astype(jnp.float32)[..., None]
    cell_count = (heights[0] * widths[0] * (channels // GROUPS)).astype(jnp.float32)
    gathered = row_major(lax.all_gather(row_major(weight), "dp", axis=0, tiled=True))
    values = latent.astype(jnp.float32) * inside
    group_total, squares = space_sum(
        (group_sum(values, GROUPS), group_sum(values * values, GROUPS)), "space"
    )
    center = group_total / cell_count
    spread = squares / cell_count - center * center
    inverse = lax.rsqrt(spread + 1e-05)
    normed = (values - spread_groups(center, channels)) * spread_groups(inverse, channels) * inside
    before = normed * norm_gain + norm_bias
    activated = (jax.nn.silu(before) * inside).astype(jnp.bfloat16)
    act_pad = pad_columns(with_halo(activated, (("space", 0),), 1))
    act_cols = jnp.concatenate(
        [
            act_pad[row_off : row_off + height_dev, col_off : col_off + width_dev]
            for row_off in range(3)
            for col_off in range(3)
        ],
        axis=-1,
    ).reshape(height_dev * width_dev, 9 * channels)
    masked = cotangent[0] * inside.astype(jnp.bfloat16)
    cot_pad = pad_columns(with_halo(masked, (("space", 0),), 1))
    flat_cot = masked.reshape(-1, channels)
    weight_terms = lax.dot_general(
        act_cols, flat_cot, (((0,), (0,)), ((), ())), preferred_element_type=jnp.float32
    ).astype(jnp.bfloat16)
    weight_terms = row_major(weight_terms)
    grad_piece, companions = halving_scatter(weight_terms, "dp", (gathered, cot_pad))
    grad_piece, (gathered, cot_pad) = replicated_sum(grad_piece, "space", companions)
    output = jnp.dot(act_cols, gathered, preferred_element_type=jnp.float32)
    block_out = (output.reshape(height_dev, width_dev, channels) * inside).astype(jnp.bfloat16)
    tap_weights = gathered.reshape(9, channels, channels)
    cot_cols = jnp.concatenate(
        [
            cot_pad[2 - row_off : 2 - row_off + height_dev, 2 - col_off : 2 - col_off + width_dev]
            for row_off in range(3)
            for col_off in range(3)
        ],
        axis=-1,
    ).reshape(height_dev * width_dev, 9 * channels)
    flipped = tap_weights.transpose(0, 2, 1).reshape(9 * channels, channels)
    upstream = jnp.dot(cot_cols, flipped, preferred_element_type=jnp.float32)
    gate_sig = jax.nn.sigmoid(before)
    silu_slope = gate_sig * (1.0 + before * (1.0 - gate_sig))
    scaled = upstream.reshape(height_dev, width_dev, channels) * silu_slope * inside * norm_gain
    local_first = group_sum(scaled, GROUPS)
    local_second = group_sum(scaled * normed, GROUPS)
    sum_first, sum_second = space_sum((local_first, local_second), "space")
    grad_piece = with_layout_constraint(grad_piece, Layout(major_to_minor=(1, 0)))
    first = sum_first / cell_count
    second = sum_second / cell_count
    input_grad = (
        spread_groups(inverse, channels)
        * (scaled - spread_groups(first, channels) - normed * spread_groups(second, channels))
        * inside
    ).astype(jnp.bfloat16)
    first_new = 0.9 * moment_one + 0.1 * grad_piece
    second_new = 0.999 * moment_two + 0.001 * grad_piece * grad_piece
    adam_update = first_new / (1.0 - 0.9**10) / (jnp.sqrt(second_new / (1.0 - 0.999**10)) + 1e-08)
    return (block_out[None], input_grad[None], grad_piece, adam_update)


def solution(mesh):
    placed = (
        P("dp", "space", None, None),
        P("dp", "space", None, None),
        P(),
        P(),
        P("dp", None),
        P("dp", None),
        P("dp", None),
        P("dp"),
        P("dp"),
    )
    return jax.shard_map(
        local,
        mesh=mesh,
        in_specs=placed,
        out_specs=(
            P("dp", "space", None, None),
            P("dp", "space", None, None),
            P("dp", None),
            P("dp", None),
        ),
        check_vma=False,
    )
```

```python
import jax
import jax.numpy as jnp
from jax import lax
from jax.experimental.layout import Layout, with_layout_constraint
from jax.sharding import PartitionSpec as P

GROUPS = 32


def with_halo(cells, sides, width):
    for axis, dim in sides:
        count = lax.axis_size(axis)
        ends = count - 1
        head = lax.slice_in_dim(cells, 0, width, axis=dim)
        tail = lax.slice_in_dim(cells, cells.shape[dim] - width, cells.shape[dim], axis=dim)
        cells = jnp.concatenate(
            [
                lax.ppermute(tail, axis, [(i, (i + 1) % count) for i in range(ends)]),
                cells,
                lax.ppermute(head, axis, [((i + 1) % count, i) for i in range(ends)]),
            ],
            axis=dim,
        )
    return cells


def space_sum(parts, axis):
    count = lax.axis_size(axis)
    if count > 4:
        return lax.psum(parts, axis)
    joined = jnp.stack(parts)
    shifted = [
        lax.ppermute(joined, axis, [(i, (i + shift) % count) for i in range(count)])
        for shift in range(1, count)
    ]
    for got in shifted:
        joined = joined + got
    return tuple(joined)


def row_major(value):
    return with_layout_constraint(value, Layout(major_to_minor=tuple(range(value.ndim))))


def halving_scatter(partial, axis, companions):
    count = lax.axis_size(axis)
    rows, channels = partial.shape[0] // count, partial.shape[1]
    if count & (count - 1):
        summed = lax.psum_scatter(
            partial.astype(jnp.bfloat16).reshape(count, rows, channels),
            axis,
            scatter_dimension=0,
            tiled=False,
        )
        return summed.astype(jnp.float32), companions
    index = lax.axis_index(axis)
    held = partial.reshape(count, rows, channels)
    step = 1
    while step < count:
        bit = (index // step) % 2
        paired = held.reshape(-1, 2, rows, channels)
        keep = lax.dynamic_index_in_dim(paired, bit, axis=1, keepdims=False)
        send = lax.dynamic_index_in_dim(paired, 1 - bit, axis=1, keepdims=False)
        pairs = [(i, i ^ step) for i in range(count)]
        got = lax.ppermute(send.astype(jnp.bfloat16), axis, pairs)
        held = (keep.astype(jnp.float32) + got.astype(jnp.float32)).astype(jnp.bfloat16)
        step *= 2
        if step < count <= 4 * step:
            break
    if step == count:
        return held[0].astype(jnp.float32), companions
    spots = count // step
    own = index // step
    total = lax.dynamic_index_in_dim(held, own, keepdims=False).astype(jnp.float32)
    for shift in range(1, spots):
        send = lax.dynamic_index_in_dim(held, own ^ shift, keepdims=False)
        pairs = [(i, i ^ (shift * step)) for i in range(count)]
        total = total + lax.ppermute(send.astype(jnp.bfloat16), axis, pairs).astype(jnp.float32)
    return total, companions


def replicated_sum(value, axis, companions):
    count = lax.axis_size(axis)
    if count & (count - 1):
        value, companions = lax.optimization_barrier((value, companions))
        return lax.psum(value.astype(jnp.bfloat16), axis).astype(jnp.float32), companions
    step = 1
    while step < count:
        mine = value.astype(jnp.bfloat16)
        pairs = [(i, i ^ step) for i in range(count)]
        value = mine.astype(jnp.float32) + lax.ppermute(mine, axis, pairs).astype(jnp.float32)
        if step == 1:
            value, companions = lax.optimization_barrier((value, companions))
        step *= 2
    return value, companions


def group_sum(values, groups):
    height_dev, width_dev, channels = values.shape
    return values.reshape(height_dev, width_dev, groups, channels // groups).sum(axis=(0, 1, 3))


def spread_groups(statistic, channels):
    return jnp.repeat(statistic, channels // statistic.shape[0])


def pad_columns(padded_rows):
    return jnp.pad(padded_rows, ((0, 0), (1, 1), (0, 0)))


def local(
    features, cotangent, norm_gain, norm_bias, weight, moment_one, moment_two, heights, widths
):
    latent = features[0]
    height_dev, width_dev, channels = latent.shape
    row_ids = lax.axis_index("space") * height_dev + jnp.arange(height_dev, dtype=jnp.int32)
    inside = (
        (row_ids < heights[0])[:, None]
        & (jnp.arange(width_dev, dtype=jnp.int32) < widths[0])[None, :]
    ).astype(jnp.float32)[..., None]
    cell_count = (heights[0] * widths[0] * (channels // GROUPS)).astype(jnp.float32)
    gathered = row_major(lax.all_gather(row_major(weight), "dp", axis=0, tiled=True))
    values = latent.astype(jnp.float32) * inside
    group_total, squares = space_sum(
        (group_sum(values, GROUPS), group_sum(values * values, GROUPS)), "space"
    )
    center = group_total / cell_count
    spread = squares / cell_count - center * center
    inverse = lax.rsqrt(spread + 1e-05)
    normed = (values - spread_groups(center, channels)) * spread_groups(inverse, channels) * inside
    before = normed * norm_gain + norm_bias
    activated = (jax.nn.silu(before) * inside).astype(jnp.bfloat16)
    act_pad = pad_columns(with_halo(activated, (("space", 0),), 1))
    act_cols = jnp.concatenate(
        [
            act_pad[row_off : row_off + height_dev, col_off : col_off + width_dev]
            for row_off in range(3)
            for col_off in range(3)
        ],
        axis=-1,
    ).reshape(height_dev * width_dev, 9 * channels)
    masked = cotangent[0] * inside.astype(jnp.bfloat16)
    cot_pad = pad_columns(with_halo(masked, (("space", 0),), 1))
    flat_cot = masked.reshape(-1, channels)
    weight_terms = lax.dot_general(
        act_cols, flat_cot, (((0,), (0,)), ((), ())), preferred_element_type=jnp.float32
    ).astype(jnp.bfloat16)
    weight_terms = row_major(weight_terms)
    grad_piece, companions = halving_scatter(weight_terms, "dp", (gathered, cot_pad))
    grad_piece, (gathered, cot_pad) = replicated_sum(grad_piece, "space", companions)
    output = jnp.dot(act_cols, gathered, preferred_element_type=jnp.float32)
    block_out = (output.reshape(height_dev, width_dev, channels) * inside).astype(jnp.bfloat16)
    tap_weights = gathered.reshape(9, channels, channels)
    cot_cols = jnp.concatenate(
        [
            cot_pad[2 - row_off : 2 - row_off + height_dev, 2 - col_off : 2 - col_off + width_dev]
            for row_off in range(3)
            for col_off in range(3)
        ],
        axis=-1,
    ).reshape(height_dev * width_dev, 9 * channels)
    upstream = lax.dot_general(
        cot_cols.reshape(-1, 9, channels),
        tap_weights,
        (((1, 2), (0, 2)), ((), ())),
        preferred_element_type=jnp.float32,
    )
    gate_sig = jax.nn.sigmoid(before)
    silu_slope = gate_sig * (1.0 + before * (1.0 - gate_sig))
    scaled = upstream.reshape(height_dev, width_dev, channels) * silu_slope * inside * norm_gain
    local_first = group_sum(scaled, GROUPS)
    local_second = group_sum(scaled * normed, GROUPS)
    sum_first, sum_second = space_sum((local_first, local_second), "space")
    grad_piece = with_layout_constraint(grad_piece, Layout(major_to_minor=(1, 0)))
    first = sum_first / cell_count
    second = sum_second / cell_count
    input_grad = (
        spread_groups(inverse, channels)
        * (scaled - spread_groups(first, channels) - normed * spread_groups(second, channels))
        * inside
    ).astype(jnp.bfloat16)
    first_new = 0.9 * moment_one + 0.1 * grad_piece
    second_new = 0.999 * moment_two + 0.001 * grad_piece * grad_piece
    adam_update = first_new / (1.0 - 0.9**10) / (jnp.sqrt(second_new / (1.0 - 0.999**10)) + 1e-08)
    return (block_out[None], input_grad[None], grad_piece, adam_update)


def solution(mesh):
    placed = (
        P("dp", "space", None, None),
        P("dp", "space", None, None),
        P(),
        P(),
        P("dp", None),
        P("dp", None),
        P("dp", None),
        P("dp"),
        P("dp"),
    )
    return jax.shard_map(
        local,
        mesh=mesh,
        in_specs=placed,
        out_specs=(
            P("dp", "space", None, None),
            P("dp", "space", None, None),
            P("dp", None),
            P("dp", None),
        ),
        check_vma=False,
    )
```

```python
import jax
import jax.numpy as jnp
from jax import lax
from jax.experimental.layout import Layout, with_layout_constraint
from jax.sharding import PartitionSpec as P

GROUPS = 32


def with_halo(cells, sides, width):
    for axis, dim in sides:
        count = lax.axis_size(axis)
        ends = count - 1
        head = lax.slice_in_dim(cells, 0, width, axis=dim)
        tail = lax.slice_in_dim(cells, cells.shape[dim] - width, cells.shape[dim], axis=dim)
        cells = jnp.concatenate(
            [
                lax.ppermute(tail, axis, [(i, (i + 1) % count) for i in range(ends)]),
                cells,
                lax.ppermute(head, axis, [((i + 1) % count, i) for i in range(ends)]),
            ],
            axis=dim,
        )
    return cells


def space_sum(parts, axis):
    count = lax.axis_size(axis)
    if count > 4:
        return lax.psum(parts, axis)
    joined = jnp.stack(parts)
    shifted = [
        lax.ppermute(joined, axis, [(i, (i + shift) % count) for i in range(count)])
        for shift in range(1, count)
    ]
    for got in shifted:
        joined = joined + got
    return tuple(joined)


def row_major(value):
    return with_layout_constraint(value, Layout(major_to_minor=tuple(range(value.ndim))))


def halving_scatter(partial, axis, companions):
    count = lax.axis_size(axis)
    rows, channels = partial.shape[0] // count, partial.shape[1]
    if count & (count - 1):
        summed = lax.psum_scatter(
            partial.astype(jnp.bfloat16).reshape(count, rows, channels),
            axis,
            scatter_dimension=0,
            tiled=False,
        )
        return summed.astype(jnp.float32), companions
    index = lax.axis_index(axis)
    held = partial.reshape(count, rows, channels)
    step = 1
    while step < count:
        bit = (index // step) % 2
        paired = held.reshape(-1, 2, rows, channels)
        keep = lax.dynamic_index_in_dim(paired, bit, axis=1, keepdims=False)
        send = lax.dynamic_index_in_dim(paired, 1 - bit, axis=1, keepdims=False)
        pairs = [(i, i ^ step) for i in range(count)]
        got = lax.ppermute(send.astype(jnp.bfloat16), axis, pairs)
        held = (keep.astype(jnp.float32) + got.astype(jnp.float32)).astype(jnp.bfloat16)
        step *= 2
        if step < count <= 4 * step:
            break
    if step == count:
        return held[0].astype(jnp.float32), companions
    spots = count // step
    own = index // step
    tied, companions = lax.optimization_barrier((held, companions))
    total = lax.dynamic_index_in_dim(tied, own, keepdims=False).astype(jnp.float32)
    for shift in range(1, spots):
        send = lax.dynamic_index_in_dim(held, own ^ shift, keepdims=False)
        pairs = [(i, i ^ (shift * step)) for i in range(count)]
        total = total + lax.ppermute(send.astype(jnp.bfloat16), axis, pairs).astype(jnp.float32)
    return total, companions


def replicated_sum(value, axis, companions):
    count = lax.axis_size(axis)
    if count & (count - 1):
        value, companions = lax.optimization_barrier((value, companions))
        return lax.psum(value.astype(jnp.bfloat16), axis).astype(jnp.float32), companions
    step = 1
    while step < count:
        mine = value.astype(jnp.bfloat16)
        pairs = [(i, i ^ step) for i in range(count)]
        value = mine.astype(jnp.float32) + lax.ppermute(mine, axis, pairs).astype(jnp.float32)
        if step == 1:
            value, companions = lax.optimization_barrier((value, companions))
        step *= 2
    return value, companions


def group_sum(values, groups):
    height_dev, width_dev, channels = values.shape
    return values.reshape(height_dev, width_dev, groups, channels // groups).sum(axis=(0, 1, 3))


def spread_groups(statistic, channels):
    return jnp.repeat(statistic, channels // statistic.shape[0])


def pad_columns(padded_rows):
    return jnp.pad(padded_rows, ((0, 0), (1, 1), (0, 0)))


def local(
    features, cotangent, norm_gain, norm_bias, weight, moment_one, moment_two, heights, widths
):
    latent = features[0]
    height_dev, width_dev, channels = latent.shape
    row_ids = lax.axis_index("space") * height_dev + jnp.arange(height_dev, dtype=jnp.int32)
    inside = (
        (row_ids < heights[0])[:, None]
        & (jnp.arange(width_dev, dtype=jnp.int32) < widths[0])[None, :]
    ).astype(jnp.float32)[..., None]
    cell_count = (heights[0] * widths[0] * (channels // GROUPS)).astype(jnp.float32)
    gathered = row_major(lax.all_gather(row_major(weight), "dp", axis=0, tiled=True))
    values = latent.astype(jnp.float32) * inside
    group_total, squares = space_sum(
        (group_sum(values, GROUPS), group_sum(values * values, GROUPS)), "space"
    )
    center = group_total / cell_count
    spread = squares / cell_count - center * center
    inverse = lax.rsqrt(spread + 1e-05)
    normed = (values - spread_groups(center, channels)) * spread_groups(inverse, channels) * inside
    before = normed * norm_gain + norm_bias
    activated = (jax.nn.silu(before) * inside).astype(jnp.bfloat16)
    act_pad = pad_columns(with_halo(activated, (("space", 0),), 1))
    act_cols = jnp.concatenate(
        [
            act_pad[row_off : row_off + height_dev, col_off : col_off + width_dev]
            for row_off in range(3)
            for col_off in range(3)
        ],
        axis=-1,
    ).reshape(height_dev * width_dev, 9 * channels)
    masked = cotangent[0] * inside.astype(jnp.bfloat16)
    cot_pad = pad_columns(with_halo(masked, (("space", 0),), 1))
    flat_cot = masked.reshape(-1, channels)
    weight_terms = lax.dot_general(
        act_cols, flat_cot, (((0,), (0,)), ((), ())), preferred_element_type=jnp.float32
    ).astype(jnp.bfloat16)
    weight_terms = row_major(weight_terms)
    grad_piece, gathered = halving_scatter(weight_terms, "dp", gathered)
    grad_piece, (gathered, cot_pad) = replicated_sum(grad_piece, "space", (gathered, cot_pad))
    output = jnp.dot(act_cols, gathered, preferred_element_type=jnp.float32)
    block_out = (output.reshape(height_dev, width_dev, channels) * inside).astype(jnp.bfloat16)
    tap_weights = gathered.reshape(9, channels, channels)
    cot_cols = jnp.concatenate(
        [
            cot_pad[2 - row_off : 2 - row_off + height_dev, 2 - col_off : 2 - col_off + width_dev]
            for row_off in range(3)
            for col_off in range(3)
        ],
        axis=-1,
    ).reshape(height_dev * width_dev, 9 * channels)
    upstream = lax.dot_general(
        cot_cols.reshape(-1, 9, channels),
        tap_weights,
        (((1, 2), (0, 2)), ((), ())),
        preferred_element_type=jnp.float32,
    )
    gate_sig = jax.nn.sigmoid(before)
    silu_slope = gate_sig * (1.0 + before * (1.0 - gate_sig))
    scaled = upstream.reshape(height_dev, width_dev, channels) * silu_slope * inside * norm_gain
    local_first = group_sum(scaled, GROUPS)
    local_second = group_sum(scaled * normed, GROUPS)
    sum_first, sum_second = space_sum((local_first, local_second), "space")
    grad_piece = with_layout_constraint(grad_piece, Layout(major_to_minor=(1, 0)))
    first = sum_first / cell_count
    second = sum_second / cell_count
    input_grad = (
        spread_groups(inverse, channels)
        * (scaled - spread_groups(first, channels) - normed * spread_groups(second, channels))
        * inside
    ).astype(jnp.bfloat16)
    first_new = 0.9 * moment_one + 0.1 * grad_piece
    second_new = 0.999 * moment_two + 0.001 * grad_piece * grad_piece
    adam_update = first_new / (1.0 - 0.9**10) / (jnp.sqrt(second_new / (1.0 - 0.999**10)) + 1e-08)
    return (block_out[None], input_grad[None], grad_piece, adam_update)


def solution(mesh):
    placed = (
        P("dp", "space", None, None),
        P("dp", "space", None, None),
        P(),
        P(),
        P("dp", None),
        P("dp", None),
        P("dp", None),
        P("dp"),
        P("dp"),
    )
    return jax.shard_map(
        local,
        mesh=mesh,
        in_specs=placed,
        out_specs=(
            P("dp", "space", None, None),
            P("dp", "space", None, None),
            P("dp", None),
            P("dp", None),
        ),
        check_vma=False,
    )
```

```python
import jax
import jax.numpy as jnp
from jax import lax
from jax.experimental.layout import Layout, with_layout_constraint
from jax.sharding import PartitionSpec as P

GROUPS = 32


def with_halo(cells, sides, width):
    for axis, dim in sides:
        count = lax.axis_size(axis)
        ends = count - 1
        head = lax.slice_in_dim(cells, 0, width, axis=dim)
        tail = lax.slice_in_dim(cells, cells.shape[dim] - width, cells.shape[dim], axis=dim)
        cells = jnp.concatenate(
            [
                lax.ppermute(tail, axis, [(i, (i + 1) % count) for i in range(ends)]),
                cells,
                lax.ppermute(head, axis, [((i + 1) % count, i) for i in range(ends)]),
            ],
            axis=dim,
        )
    return cells


def space_sum(parts, axis):
    count = lax.axis_size(axis)
    if count > 4:
        return lax.psum(parts, axis)
    joined = jnp.stack(parts)
    shifted = [
        lax.ppermute(joined, axis, [(i, (i + shift) % count) for i in range(count)])
        for shift in range(1, count)
    ]
    for got in shifted:
        joined = joined + got
    return tuple(joined)


def row_major(value):
    return with_layout_constraint(value, Layout(major_to_minor=tuple(range(value.ndim))))


def halving_scatter(partial, axis, companions):
    count = lax.axis_size(axis)
    rows, channels = partial.shape[0] // count, partial.shape[1]
    if count & (count - 1):
        summed = lax.psum_scatter(
            partial.astype(jnp.bfloat16).reshape(count, rows, channels),
            axis,
            scatter_dimension=0,
            tiled=False,
        )
        return summed.astype(jnp.float32), companions
    index = lax.axis_index(axis)
    held = partial.reshape(count, rows, channels)
    step = 1
    while step < count:
        bit = (index // step) % 2
        paired = held.reshape(-1, 2, rows, channels)
        keep = lax.dynamic_index_in_dim(paired, bit, axis=1, keepdims=False)
        send = lax.dynamic_index_in_dim(paired, 1 - bit, axis=1, keepdims=False)
        pairs = [(i, i ^ step) for i in range(count)]
        got = lax.ppermute(send.astype(jnp.bfloat16), axis, pairs)
        held = (keep.astype(jnp.float32) + got.astype(jnp.float32)).astype(jnp.bfloat16)
        step *= 2
        if step < count <= 4 * step:
            break
    if step == count:
        return held[0].astype(jnp.float32), companions
    spots = count // step
    own = index // step
    tied, companions = lax.optimization_barrier((held, companions))
    total = lax.dynamic_index_in_dim(tied, own, keepdims=False).astype(jnp.float32)
    for shift in range(1, spots):
        send = lax.dynamic_index_in_dim(held, own ^ shift, keepdims=False)
        pairs = [(i, i ^ (shift * step)) for i in range(count)]
        total = total + lax.ppermute(send.astype(jnp.bfloat16), axis, pairs).astype(jnp.float32)
    return total, companions


def replicated_sum(value, axis, companions):
    count = lax.axis_size(axis)
    if count & (count - 1):
        value, companions = lax.optimization_barrier((value, companions))
        return lax.psum(value.astype(jnp.bfloat16), axis).astype(jnp.float32), companions
    step = 1
    while step < count:
        mine = value.astype(jnp.bfloat16)
        pairs = [(i, i ^ step) for i in range(count)]
        value = mine.astype(jnp.float32) + lax.ppermute(mine, axis, pairs).astype(jnp.float32)
        if step == 1:
            value, companions = lax.optimization_barrier((value, companions))
        step *= 2
    return value, companions


def group_sum(values, groups):
    height_dev, width_dev, channels = values.shape
    return values.reshape(height_dev, width_dev, groups, channels // groups).sum(axis=(0, 1, 3))


def spread_groups(statistic, channels):
    return jnp.repeat(statistic, channels // statistic.shape[0])


def pad_columns(padded_rows):
    return jnp.pad(padded_rows, ((0, 0), (1, 1), (0, 0)))


def local(
    features, cotangent, norm_gain, norm_bias, weight, moment_one, moment_two, heights, widths
):
    latent = features[0]
    height_dev, width_dev, channels = latent.shape
    row_ids = lax.axis_index("space") * height_dev + jnp.arange(height_dev, dtype=jnp.int32)
    inside = (
        (row_ids < heights[0])[:, None]
        & (jnp.arange(width_dev, dtype=jnp.int32) < widths[0])[None, :]
    ).astype(jnp.float32)[..., None]
    cell_count = (heights[0] * widths[0] * (channels // GROUPS)).astype(jnp.float32)
    gathered = row_major(lax.all_gather(row_major(weight), "dp", axis=0, tiled=True))
    values = latent.astype(jnp.float32) * inside
    group_total, squares = space_sum(
        (group_sum(values, GROUPS), group_sum(values * values, GROUPS)), "space"
    )
    center = group_total / cell_count
    spread = squares / cell_count - center * center
    inverse = lax.rsqrt(spread + 1e-05)
    normed = (values - spread_groups(center, channels)) * spread_groups(inverse, channels) * inside
    before = normed * norm_gain + norm_bias
    activated = (jax.nn.silu(before) * inside).astype(jnp.bfloat16)
    act_pad = pad_columns(with_halo(activated, (("space", 0),), 1))
    act_cols = jnp.concatenate(
        [
            act_pad[row_off : row_off + height_dev, col_off : col_off + width_dev]
            for row_off in range(3)
            for col_off in range(3)
        ],
        axis=-1,
    ).reshape(height_dev * width_dev, 9 * channels)
    masked = cotangent[0] * inside.astype(jnp.bfloat16)
    cot_pad = pad_columns(with_halo(masked, (("space", 0),), 1))
    flat_cot = masked.reshape(-1, channels)
    weight_terms = lax.dot_general(
        act_cols, flat_cot, (((0,), (0,)), ((), ())), preferred_element_type=jnp.float32
    ).astype(jnp.bfloat16)
    weight_terms = row_major(weight_terms)
    output = jnp.dot(act_cols, gathered, preferred_element_type=jnp.float32)
    block_out = (output.reshape(height_dev, width_dev, channels) * inside).astype(jnp.bfloat16)
    grad_piece, (gathered, block_out) = halving_scatter(weight_terms, "dp", (gathered, block_out))
    grad_piece, (gathered, cot_pad) = replicated_sum(grad_piece, "space", (gathered, cot_pad))
    tap_weights = gathered.reshape(9, channels, channels)
    cot_cols = jnp.concatenate(
        [
            cot_pad[2 - row_off : 2 - row_off + height_dev, 2 - col_off : 2 - col_off + width_dev]
            for row_off in range(3)
            for col_off in range(3)
        ],
        axis=-1,
    ).reshape(height_dev * width_dev, 9 * channels)
    upstream = lax.dot_general(
        cot_cols.reshape(-1, 9, channels),
        tap_weights,
        (((1, 2), (0, 2)), ((), ())),
        preferred_element_type=jnp.float32,
    )
    gate_sig = jax.nn.sigmoid(before)
    silu_slope = gate_sig * (1.0 + before * (1.0 - gate_sig))
    scaled = upstream.reshape(height_dev, width_dev, channels) * silu_slope * inside * norm_gain
    local_first = group_sum(scaled, GROUPS)
    local_second = group_sum(scaled * normed, GROUPS)
    sum_first, sum_second = space_sum((local_first, local_second), "space")
    grad_piece = with_layout_constraint(grad_piece, Layout(major_to_minor=(1, 0)))
    first = sum_first / cell_count
    second = sum_second / cell_count
    input_grad = (
        spread_groups(inverse, channels)
        * (scaled - spread_groups(first, channels) - normed * spread_groups(second, channels))
        * inside
    ).astype(jnp.bfloat16)
    first_new = 0.9 * moment_one + 0.1 * grad_piece
    second_new = 0.999 * moment_two + 0.001 * grad_piece * grad_piece
    adam_update = first_new / (1.0 - 0.9**10) / (jnp.sqrt(second_new / (1.0 - 0.999**10)) + 1e-08)
    return (block_out[None], input_grad[None], grad_piece, adam_update)


def solution(mesh):
    placed = (
        P("dp", "space", None, None),
        P("dp", "space", None, None),
        P(),
        P(),
        P("dp", None),
        P("dp", None),
        P("dp", None),
        P("dp"),
        P("dp"),
    )
    return jax.shard_map(
        local,
        mesh=mesh,
        in_specs=placed,
        out_specs=(
            P("dp", "space", None, None),
            P("dp", "space", None, None),
            P("dp", None),
            P("dp", None),
        ),
        check_vma=False,
    )
```

```python
import jax
import jax.numpy as jnp
from jax import lax
from jax.experimental.layout import Layout, with_layout_constraint
from jax.sharding import PartitionSpec as P

GROUPS = 32


def with_halo(cells, sides, width):
    for axis, dim in sides:
        count = lax.axis_size(axis)
        ends = count - 1
        head = lax.slice_in_dim(cells, 0, width, axis=dim)
        tail = lax.slice_in_dim(cells, cells.shape[dim] - width, cells.shape[dim], axis=dim)
        cells = jnp.concatenate(
            [
                lax.ppermute(tail, axis, [(i, (i + 1) % count) for i in range(ends)]),
                cells,
                lax.ppermute(head, axis, [((i + 1) % count, i) for i in range(ends)]),
            ],
            axis=dim,
        )
    return cells


def space_sum(parts, axis):
    count = lax.axis_size(axis)
    if count > 4:
        return lax.psum(parts, axis)
    joined = jnp.stack(parts)
    shifted = [
        lax.ppermute(joined, axis, [(i, (i + shift) % count) for i in range(count)])
        for shift in range(1, count)
    ]
    for got in shifted:
        joined = joined + got
    return tuple(joined)


def row_major(value):
    return with_layout_constraint(value, Layout(major_to_minor=tuple(range(value.ndim))))


def halving_scatter(partial, axis, companions):
    count = lax.axis_size(axis)
    rows, channels = partial.shape[0] // count, partial.shape[1]
    if count & (count - 1):
        summed = lax.psum_scatter(
            partial.astype(jnp.bfloat16).reshape(count, rows, channels),
            axis,
            scatter_dimension=0,
            tiled=False,
        )
        return summed.astype(jnp.float32), companions
    index = lax.axis_index(axis)
    held = partial.reshape(count, rows, channels)
    step = 1
    while step < count:
        bit = (index // step) % 2
        paired = held.reshape(-1, 2, rows, channels)
        keep = lax.dynamic_index_in_dim(paired, bit, axis=1, keepdims=False)
        send = lax.dynamic_index_in_dim(paired, 1 - bit, axis=1, keepdims=False)
        pairs = [(i, i ^ step) for i in range(count)]
        got = lax.ppermute(send.astype(jnp.bfloat16), axis, pairs)
        held = (keep.astype(jnp.float32) + got.astype(jnp.float32)).astype(jnp.bfloat16)
        step *= 2
        if step < count <= 4 * step:
            break
    if step == count:
        return held[0].astype(jnp.float32), companions
    spots = count // step
    own = index // step
    tied, companions = lax.optimization_barrier((held, companions))
    total = lax.dynamic_index_in_dim(tied, own, keepdims=False).astype(jnp.float32)
    for shift in range(1, spots):
        send = lax.dynamic_index_in_dim(held, own ^ shift, keepdims=False)
        pairs = [(i, i ^ (shift * step)) for i in range(count)]
        total = total + lax.ppermute(send.astype(jnp.bfloat16), axis, pairs).astype(jnp.float32)
    return total, companions


def replicated_sum(value, axis, companions):
    count = lax.axis_size(axis)
    if count & (count - 1):
        value, companions = lax.optimization_barrier((value, companions))
        return lax.psum(value.astype(jnp.bfloat16), axis).astype(jnp.float32), companions
    step = 1
    while step < count:
        mine = value.astype(jnp.bfloat16)
        pairs = [(i, i ^ step) for i in range(count)]
        value = mine.astype(jnp.float32) + lax.ppermute(mine, axis, pairs).astype(jnp.float32)
        if step == 1:
            value, companions = lax.optimization_barrier((value, companions))
        step *= 2
    return value, companions


def group_sum(values, groups):
    height_dev, width_dev, channels = values.shape
    return values.reshape(height_dev, width_dev, groups, channels // groups).sum(axis=(0, 1, 3))


def spread_groups(statistic, channels):
    return jnp.repeat(statistic, channels // statistic.shape[0])


def pad_columns(padded_rows):
    return jnp.pad(padded_rows, ((0, 0), (1, 1), (0, 0)))


def local(
    features, cotangent, norm_gain, norm_bias, weight, moment_one, moment_two, heights, widths
):
    latent = features[0]
    height_dev, width_dev, channels = latent.shape
    row_ids = lax.axis_index("space") * height_dev + jnp.arange(height_dev, dtype=jnp.int32)
    inside = (
        (row_ids < heights[0])[:, None]
        & (jnp.arange(width_dev, dtype=jnp.int32) < widths[0])[None, :]
    ).astype(jnp.float32)[..., None]
    cell_count = (heights[0] * widths[0] * (channels // GROUPS)).astype(jnp.float32)
    gathered = row_major(lax.all_gather(row_major(weight), "dp", axis=0, tiled=True))
    values = latent.astype(jnp.float32) * inside
    group_total, squares = space_sum(
        (group_sum(values, GROUPS), group_sum(values * values, GROUPS)), "space"
    )
    center = group_total / cell_count
    spread = squares / cell_count - center * center
    inverse = lax.rsqrt(spread + 1e-05)
    normed = (values - spread_groups(center, channels)) * spread_groups(inverse, channels) * inside
    before = normed * norm_gain + norm_bias
    activated = (jax.nn.silu(before) * inside).astype(jnp.bfloat16)
    act_pad = pad_columns(with_halo(activated, (("space", 0),), 1))
    act_cols = jnp.concatenate(
        [
            act_pad[row_off : row_off + height_dev, col_off : col_off + width_dev]
            for row_off in range(3)
            for col_off in range(3)
        ],
        axis=-1,
    ).reshape(height_dev * width_dev, 9 * channels)
    masked = cotangent[0] * inside.astype(jnp.bfloat16)
    cot_pad = pad_columns(with_halo(masked, (("space", 0),), 1))
    flat_cot = masked.reshape(-1, channels)
    weight_terms = lax.dot_general(
        act_cols, flat_cot, (((0,), (0,)), ((), ())), preferred_element_type=jnp.float32
    ).astype(jnp.bfloat16)
    weight_terms = row_major(weight_terms)
    output = jnp.dot(act_cols, gathered, preferred_element_type=jnp.float32)
    block_out = (output.reshape(height_dev, width_dev, channels) * inside).astype(jnp.bfloat16)
    grad_piece, (gathered, block_out) = halving_scatter(weight_terms, "dp", (gathered, block_out))
    tap_weights = gathered.reshape(9, channels, channels)
    cot_cols = jnp.concatenate(
        [
            cot_pad[2 - row_off : 2 - row_off + height_dev, 2 - col_off : 2 - col_off + width_dev]
            for row_off in range(3)
            for col_off in range(3)
        ],
        axis=-1,
    ).reshape(height_dev * width_dev, 9 * channels)
    upstream = lax.dot_general(
        cot_cols.reshape(-1, 9, channels),
        tap_weights,
        (((1, 2), (0, 2)), ((), ())),
        preferred_element_type=jnp.float32,
    )
    grad_piece, upstream = replicated_sum(grad_piece, "space", upstream)
    gate_sig = jax.nn.sigmoid(before)
    silu_slope = gate_sig * (1.0 + before * (1.0 - gate_sig))
    scaled = upstream.reshape(height_dev, width_dev, channels) * silu_slope * inside * norm_gain
    local_first = group_sum(scaled, GROUPS)
    local_second = group_sum(scaled * normed, GROUPS)
    sum_first, sum_second = space_sum((local_first, local_second), "space")
    grad_piece = with_layout_constraint(grad_piece, Layout(major_to_minor=(1, 0)))
    first = sum_first / cell_count
    second = sum_second / cell_count
    input_grad = (
        spread_groups(inverse, channels)
        * (scaled - spread_groups(first, channels) - normed * spread_groups(second, channels))
        * inside
    ).astype(jnp.bfloat16)
    first_new = 0.9 * moment_one + 0.1 * grad_piece
    second_new = 0.999 * moment_two + 0.001 * grad_piece * grad_piece
    adam_update = first_new / (1.0 - 0.9**10) / (jnp.sqrt(second_new / (1.0 - 0.999**10)) + 1e-08)
    return (block_out[None], input_grad[None], grad_piece, adam_update)


def solution(mesh):
    placed = (
        P("dp", "space", None, None),
        P("dp", "space", None, None),
        P(),
        P(),
        P("dp", None),
        P("dp", None),
        P("dp", None),
        P("dp"),
        P("dp"),
    )
    return jax.shard_map(
        local,
        mesh=mesh,
        in_specs=placed,
        out_specs=(
            P("dp", "space", None, None),
            P("dp", "space", None, None),
            P("dp", None),
            P("dp", None),
        ),
        check_vma=False,
    )
```
